256 devices in a mesh: space: 32 (over z_hi, x, core), scen: 8 (over y, z_lo).
Axes of the slice: x: 4, y: 4, z: 8 (z_hi: 4, z_lo: 2; z = z_hi * 2 + z_lo), core: 2. Of those that a mesh axis runs over, the one named last changes fastest.
Arguments:
- concentration: float32 [8, 8, 6, 384, 384], P('scen', None, None, 'space'), may hold values from -6 to 6
- emissions: float32 [8, 6, 384, 384], P('scen', None, 'space'), may hold values from -3 to 3
- courant: float32 [2, 8, 6, 384, 384], P(None, None, None, 'space'), may hold values from -0.9 to 0.9
- tile_source: int32 [8640], P('space'), may hold values from 0 to 215, as said below
- tile_target: int32 [8640], P('space'), may hold values from 0 to 1023, as said below
- intersection: bfloat16 [8640, 128, 128], P('space'), may hold values from 0 to 0.0625
Outputs:
- transported: float32 [8, 8, 6, 384, 384], P('scen', None, None, 'space')
- regridded: float32 [8, 8, 1024, 128], P('scen', None, 'space')
- ensemble_moments: float32 [2, 8, 1024, 128], P(None, None, 'space')
The draws below stay inside these ranges and needn't reach their ends.
Inputs may be any that keep to these rules, and one draw needn't show every extreme that they name: `tile_source`: every source block of a row band is named by at least one of the band's tiles. `tile_target`: latitude band b holds target blocks b * 32 to (b+1) * 32 - 1. The 270 tiles of one row band name at most 16 blocks of any one latitude band and at least 8 of every latitude band but one, which receives exactly 16 tiles from every row band. Every target block is named by some tile.
All inputs are finite; a program needn't handle non-finite values.
Results may differ from the reference program's by a relative error of at most 0.0027.
Values sent between devices are 32-bit elements; how exact they have to be, the bound alone decides.
No kernel may reach another device: no remote copies, remote signals or barrier semaphores. Data moves between devices by JAX's collectives and lax.ppermute only.
A program may use at most 128 MiB of HBM per device.

```python
import jax
import jax.numpy as jnp
from jax import lax

LEV = 8
C = 384
BLK = 128
TGT_DEV = 32
R = 12
BANDS = 32
SCEN = 8
TILES_DEV = 270
CAP = 16
BASE = 8
TGT_BLKS = 1024


def draw_tile_source(key, part):
    blocks = 6 * R * C // BLK

    def one_band(band_key):
        first_key, second_key, third_key = jax.random.split(band_key, 3)
        covered = jax.random.permutation(first_key, blocks).astype(jnp.int32)
        extra_blocks = jax.random.randint(second_key, (TILES_DEV - blocks,), 0, blocks).astype(jnp.int32)
        return jax.random.permutation(third_key, jnp.concatenate([covered, extra_blocks]))
    band_keys = jax.random.split(jax.random.fold_in(key, 3), BANDS)
    return jax.vmap(one_band)(band_keys).reshape(-1).astype(jnp.int32)


def draw_tile_target(key, part):
    hot_key, band_key, order_key = jax.random.split(jax.random.fold_in(key, 5), 3)
    hottest = jax.random.randint(hot_key, (), 0, BANDS).astype(jnp.int32)
    others = jnp.arange(BANDS - 1, dtype=jnp.int32)
    others = others + (others >= hottest).astype(jnp.int32)
    spare_count = TILES_DEV - CAP - (BANDS - 1) * BASE

    def one_band(single_key):
        pick_key, mix_key = jax.random.split(single_key)
        candidates = jnp.repeat(others, CAP - BASE)
        chosen = jax.random.permutation(pick_key, candidates)[:spare_count]
        owners = jnp.concatenate([jnp.full((CAP,), hottest, jnp.int32), jnp.repeat(others, BASE), chosen.astype(jnp.int32)])
        return jax.random.permutation(mix_key, owners)
    owners = jax.vmap(one_band)(jax.random.split(band_key, BANDS)).reshape(-1).astype(jnp.int32)
    marked = (owners[:, None] == jnp.arange(BANDS, dtype=jnp.int32)[None, :]).astype(jnp.int32)
    ranking = jnp.sum((jnp.cumsum(marked, axis=0) - marked) * marked, axis=1).astype(jnp.int32)

    def one_table(single_key):
        return jax.random.permutation(single_key, TGT_DEV).astype(jnp.int32)
    tables = jax.vmap(one_table)(jax.random.split(order_key, BANDS))
    blocks = tables[owners, ranking % TGT_DEV]
    return (owners * TGT_DEV + blocks).astype(jnp.int32)


def shard_levels(key, dims, shards, smallest, largest):
    def one(dim, blocks):
        draws = jax.random.uniform(jax.random.fold_in(jax.random.fold_in(key, 6), dim), (blocks,), jnp.float32, smallest / len(shards), largest / len(shards))
        return jnp.repeat(jnp.exp(draws), dims[dim] // blocks).reshape((-1,) + (1,) * (len(dims) - dim - 1))

    loudness = one(*shards[0])
    for cut in shards[1:]:
        loudness = loudness * one(*cut)
    return loudness


def scatter_about(stream_key, dims, spread, reach, shards=(), kind=jnp.bfloat16):
    values = spread * jax.random.normal(stream_key, dims, jnp.float32)
    if shards:
        values = values * shard_levels(stream_key, dims, shards, -0.22, 0.18)
    return jnp.clip(values, -reach, reach).astype(kind)


def setup_inputs(seed: int = 0) -> dict:
    key_list = jax.random.split(jax.random.key(seed), 7)
    concentration = scatter_about(key_list[0], (SCEN, LEV, 6, C, C), 1.0, 6.0, ((0, 8), (3, 32)), jnp.float32)
    emissions = scatter_about(key_list[1], (SCEN, 6, C, C), 0.5, 3.0, ((0, 8), (2, 32)), jnp.float32)
    courant = jnp.clip(jax.random.uniform(key_list[2], (2, LEV, 6, C, C), jnp.float32, -0.9, 0.9) * shard_levels(key_list[2], (2, LEV, 6, C, C), ((3, 32),), -0.4, 0.0), -0.9, 0.9)
    tile_source = draw_tile_source(jax.random.fold_in(key_list[6], 71), 0)
    tile_target = draw_tile_target(jax.random.fold_in(key_list[6], 71), 0)
    intersection = jnp.clip(0.0625 * jax.random.uniform(key_list[5], (TILES_DEV * BANDS, BLK, BLK), jnp.float32) ** shard_levels(key_list[5], (TILES_DEV * BANDS, BLK, BLK), ((0, 32),), -0.2, 0.2), 0.0, 0.0625).astype(jnp.bfloat16)
    return dict(concentration=concentration, emissions=emissions, courant=courant, tile_source=tile_source, tile_target=tile_target, intersection=intersection)


def parabola_sweep(padded, courant_faces, sweep_axis):
    cells_along = padded.shape[sweep_axis] - 6

    def window(values_in, first_cell, length):
        return lax.slice_in_dim(values_in, first_cell, first_cell + length, axis=sweep_axis)

    edge_values = (7.0 / 12.0) * (window(padded, 1, cells_along + 3) + window(padded, 2, cells_along + 3)) - (1.0 / 12.0) * (window(padded, 0, cells_along + 3) + window(padded, 3, cells_along + 3))
    left_edge = window(edge_values, 0, cells_along + 2)
    right_edge = window(edge_values, 1, cells_along + 2)
    centre = window(padded, 2, cells_along + 2)
    slopes = right_edge - left_edge
    curvature = 6.0 * centre - 3.0 * (left_edge + right_edge)
    backward = -courant_faces
    upwind_left = courant_faces * (window(right_edge, 0, cells_along + 1) - 0.5 * courant_faces * (window(slopes, 0, cells_along + 1) - (1.0 - 2.0 * courant_faces / 3.0) * window(curvature, 0, cells_along + 1)))
    upwind_right = courant_faces * (window(left_edge, 1, cells_along + 1) + 0.5 * backward * (window(slopes, 1, cells_along + 1) + (1.0 - 2.0 * backward / 3.0) * window(curvature, 1, cells_along + 1)))
    fluxes = jnp.where(courant_faces >= 0.0, upwind_left, upwind_right)
    return window(padded, 3, cells_along) - (window(fluxes, 1, cells_along) - window(fluxes, 0, cells_along))


def column_pad(tracer, east_wind, north_wind):
    padded_faces = []
    speed_faces = []
    for face_number in range(6):
        if face_number % 2 == 0:
            source = tracer[:, (face_number - 2) % 6, C - 3:, :]
            west_cells = jnp.swapaxes(jnp.flip(source, -1), -1, -2)
            west_speed = jnp.flip(north_wind[:, (face_number - 2) % 6, C - 1, :], -1)
            east_cells = tracer[:, (face_number + 1) % 6, :, 0:3]
            east_speed = east_wind[:, (face_number + 1) % 6, :, 0]
        else:
            west_cells = tracer[:, (face_number - 1) % 6, :, C - 3:]
            west_speed = east_wind[:, (face_number - 1) % 6, :, C - 1]
            source = tracer[:, (face_number + 2) % 6, 0:3, :]
            east_cells = jnp.swapaxes(jnp.flip(source, -1), -1, -2)
            east_speed = jnp.flip(north_wind[:, (face_number + 2) % 6, 0, :], -1)
        padded_faces.append(jnp.concatenate([west_cells, tracer[:, face_number], east_cells], -1))
        speeds = jnp.concatenate([west_speed[:, :, None], east_wind[:, face_number], east_speed[:, :, None]], -1)
        speed_faces.append(0.5 * (speeds[:, :, :-1] + speeds[:, :, 1:]))
    return jnp.stack(padded_faces, 1), jnp.stack(speed_faces, 1)


def row_pad(tracer, east_wind, north_wind):
    padded_faces = []
    speed_faces = []
    for face_number in range(6):
        if face_number % 2 == 0:
            north_cells = jnp.swapaxes(jnp.flip(tracer[:, (face_number + 2) % 6, :, 0:3], -2), -1, -2)
            north_speed = jnp.flip(east_wind[:, (face_number + 2) % 6, :, 0], -1)
            south_cells = tracer[:, (face_number - 1) % 6, C - 3:, :]
            south_speed = north_wind[:, (face_number - 1) % 6, C - 1, :]
        else:
            north_cells = tracer[:, (face_number + 1) % 6, 0:3, :]
            north_speed = north_wind[:, (face_number + 1) % 6, 0, :]
            south_cells = jnp.swapaxes(jnp.flip(tracer[:, (face_number - 2) % 6, :, C - 3:], -2), -1, -2)
            south_speed = jnp.flip(east_wind[:, (face_number - 2) % 6, :, C - 1], -1)
        padded_faces.append(jnp.concatenate([south_cells, tracer[:, face_number], north_cells], -2))
        speeds = jnp.concatenate([south_speed[:, None, :], north_wind[:, face_number], north_speed[:, None, :]], -2)
        speed_faces.append(0.5 * (speeds[:, :-1, :] + speeds[:, 1:, :]))
    return jnp.stack(padded_faces, 1), jnp.stack(speed_faces, 1)


def reference(concentration, emissions, courant, tile_source, tile_target, intersection):
    east_wind = courant[0]
    north_wind = courant[1]

    def advance(scenario_pair):
        tracer = scenario_pair[0].at[0].add(scenario_pair[1])
        for step_number in range(2):
            padded, courant_faces = column_pad(tracer, east_wind, north_wind)
            tracer = parabola_sweep(padded, courant_faces, 3)
            padded, courant_faces = row_pad(tracer, east_wind, north_wind)
            tracer = parabola_sweep(padded, courant_faces, 2)
        return tracer

    transported = lax.map(advance, (concentration, emissions))

    def add_band(band_number, accumulated):
        start_row = (band_number * R).astype(jnp.int32)
        start_tile = (band_number * TILES_DEV).astype(jnp.int32)
        rows_taken = lax.dynamic_slice_in_dim(transported, start_row, R, axis=3)
        rounded = lax.optimization_barrier(rows_taken.astype(jnp.bfloat16)).astype(jnp.float32)
        blocks = rounded.reshape(SCEN * LEV, -1, BLK)
        sources = lax.dynamic_slice_in_dim(tile_source, start_tile, TILES_DEV).astype(jnp.int32)
        targets = lax.dynamic_slice_in_dim(tile_target, start_tile, TILES_DEV).astype(jnp.int32)
        weights = lax.dynamic_slice_in_dim(intersection, start_tile, TILES_DEV, axis=0).astype(jnp.float32)
        chosen = jnp.take(blocks, sources, axis=1)
        partial_value = jnp.einsum("btk,tkc->btc", chosen, weights, precision=lax.Precision.HIGHEST)
        return accumulated.at[:, targets].add(partial_value)

    accumulated = lax.fori_loop(0, BANDS, add_band, jnp.zeros((SCEN * LEV, TGT_BLKS, BLK), jnp.float32))
    regridded = accumulated.reshape(SCEN, LEV, TGT_BLKS, BLK)
    moments = jnp.stack([jnp.sum(regridded, 0), jnp.sum(regridded * regridded, 0)]) / SCEN
    return transported, regridded, moments
```

```python
import jax
import jax.numpy as jnp
from jax import lax
from jax.sharding import PartitionSpec as P

TGT_DEV = 32
SLOTS = 16


def from_behind(block, axis, distance):
    devices = range(lax.axis_size(axis))
    route = [((i - distance) % len(devices), i) for i in devices]
    return lax.ppermute(block, axis, route)


def parabola_sweep(padded, courant_faces, sweep_axis):
    cells_along = padded.shape[sweep_axis] - 6

    def window(values_in, first_cell, length):
        return lax.slice_in_dim(values_in, first_cell, first_cell + length, axis=sweep_axis)

    edge_values = 7.0 / 12.0 * (
        window(padded, 1, cells_along + 3) + window(padded, 2, cells_along + 3)
    ) - 1.0 / 12.0 * (window(padded, 0, cells_along + 3) + window(padded, 3, cells_along + 3))
    left_edge = window(edge_values, 0, cells_along + 2)
    right_edge = window(edge_values, 1, cells_along + 2)
    centre = window(padded, 2, cells_along + 2)
    slopes = right_edge - left_edge
    curvature = 6.0 * centre - 3.0 * (left_edge + right_edge)
    backward = -courant_faces
    upwind_left = courant_faces * (
        window(right_edge, 0, cells_along + 1)
        - 0.5
        * courant_faces
        * (
            window(slopes, 0, cells_along + 1)
            - (1.0 - 2.0 * courant_faces / 3.0) * window(curvature, 0, cells_along + 1)
        )
    )
    upwind_right = courant_faces * (
        window(left_edge, 1, cells_along + 1)
        + 0.5
        * backward
        * (
            window(slopes, 1, cells_along + 1)
            + (1.0 - 2.0 * backward / 3.0) * window(curvature, 1, cells_along + 1)
        )
    )
    fluxes = jnp.where(courant_faces >= 0.0, upwind_left, upwind_right)
    return window(padded, 3, cells_along) - (
        window(fluxes, 1, cells_along) - window(fluxes, 0, cells_along)
    )


def by_destination(values, band_count):
    width = values.shape[-1]
    blocks = values.reshape(values.shape[:-1] + (band_count, width // band_count))
    return jnp.flip(jnp.moveaxis(blocks, -2, 0), 0).reshape(band_count, -1)


def pack_rows(tracer, north_wind, lowest):
    row_count = tracer.shape[3]
    width_cells = tracer.shape[4]
    if lowest:
        layers = tracer[:, :, :, 0:3, :]
    else:
        layers = tracer[:, :, :, row_count - 3 :, :]
    parts = [layers.reshape(-1, width_cells)]
    if north_wind is not None:
        wind_row = north_wind[:, :, 0:1, :] if lowest else north_wind[:, :, row_count - 1 :, :]
        parts.append(wind_row.reshape(-1, width_cells))
    return jnp.concatenate(parts, 0)


def edge_rows(tracer, north_wind, position, band_count, with_wind):
    row_count = tracer.shape[3]
    top_parts = [by_destination(tracer[:, :, 0::2, row_count - 3 :, :], band_count)]
    low_parts = [by_destination(tracer[:, :, 1::2, 0:3, :], band_count)]
    if with_wind:
        top_parts.append(by_destination(north_wind[:, 0::2, row_count - 1, :], band_count))
        low_parts.append(by_destination(north_wind[:, 1::2, 0, :], band_count))
    send_top = jnp.concatenate(top_parts, 1)
    send_low = jnp.concatenate(low_parts, 1)
    send = jnp.where(
        position == band_count - 1, send_top, jnp.where(position == 0, send_low, 0.0)
    ).astype(send_top.dtype)
    got = lax.all_to_all(send, "space", 0, 0, tiled=True)
    return got[band_count - 1], got[0]


def column_halos(tracer, east_wind, north_wind, position, band_count, edge_wind):
    scenarios, levels, _, row_count, width_cells = tracer.shape
    top, low = edge_rows(tracer, north_wind, position, band_count, edge_wind is None)
    cells = scenarios * levels * 3 * 3 * row_count
    top_layers = top[:cells].reshape(scenarios, levels, 3, 3, row_count)
    low_layers = low[:cells].reshape(scenarios, levels, 3, 3, row_count)
    if edge_wind is None:
        edge_wind = (
            top[cells:].reshape(levels, 3, row_count),
            low[cells:].reshape(levels, 3, row_count),
        )
    top_wind, low_wind = edge_wind
    padded_faces = []
    speed_faces = []
    for face_number in range(6):
        half = face_number // 2
        if face_number % 2 == 0:
            source = top_layers[:, :, (half - 1) % 3]
            west_cells = jnp.swapaxes(jnp.flip(source, -1), -1, -2)
            west_speed = jnp.flip(top_wind[:, (half - 1) % 3], -1)
            east_cells = tracer[:, :, (face_number + 1) % 6, :, 0:3]
            east_speed = east_wind[:, (face_number + 1) % 6, :, 0]
        else:
            west_cells = tracer[:, :, (face_number - 1) % 6, :, width_cells - 3 :]
            west_speed = east_wind[:, (face_number - 1) % 6, :, width_cells - 1]
            source = low_layers[:, :, (half + 1) % 3]
            east_cells = jnp.swapaxes(jnp.flip(source, -1), -1, -2)
            east_speed = jnp.flip(low_wind[:, (half + 1) % 3], -1)
        padded_faces.append(
            jnp.concatenate([west_cells, tracer[:, :, face_number], east_cells], -1)
        )
        speeds = jnp.concatenate(
            [west_speed[:, :, None], east_wind[:, face_number], east_speed[:, :, None]], -1
        )
        speed_faces.append(0.5 * (speeds[:, :, :-1] + speeds[:, :, 1:]))
    return (jnp.stack(padded_faces, 2), jnp.stack(speed_faces, 1), edge_wind)


def edge_columns(tracer, east_wind, position, band_count, with_wind):
    scenarios, levels, _, row_count, width_cells = tracer.shape
    to_top = [jnp.swapaxes(tracer[:, :, 0::2, :, 0:3], -1, -2).reshape(-1)]
    to_low = [jnp.swapaxes(tracer[:, :, 1::2, :, width_cells - 3 :], -1, -2).reshape(-1)]
    if with_wind:
        to_top.append(east_wind[:, 0::2, :, 0].reshape(-1))
        to_low.append(east_wind[:, 1::2, :, width_cells - 1].reshape(-1))
    to_top = jnp.concatenate(to_top)
    to_low = jnp.concatenate(to_low)
    send = jnp.zeros((band_count,) + to_top.shape, to_top.dtype)
    send = send.at[band_count - 1].set(to_top).at[0].set(to_low)
    got = lax.all_to_all(send, "space", 0, 0, tiled=True)
    cells = scenarios * levels * 3 * 3 * row_count
    layers = got[:, :cells].reshape(band_count, scenarios, levels, 3, 3, row_count)
    layers = jnp.moveaxis(layers, 0, -2).reshape(scenarios, levels, 3, 3, band_count * row_count)
    wind = None
    if with_wind:
        wind = got[:, cells:].reshape(band_count, levels, 3, row_count)
        wind = jnp.moveaxis(wind, 0, -2).reshape(levels, 3, band_count * row_count)
    return layers, wind


def row_halos(tracer, east_wind, north_wind, position, band_count, row_wind):
    first_step = row_wind is None
    shifted = []
    for step_by, lowest in ((-1, True), (1, False)):
        packed = pack_rows(tracer, north_wind if first_step else None, lowest)
        shifted.append(from_behind(packed, "space", step_by))
    edge_layers, edge_speed = edge_columns(tracer, east_wind, position, band_count, first_step)
    layer_rows = tracer.shape[0] * tracer.shape[1] * 18
    width_cells = tracer.shape[4]
    if first_step:
        levels = tracer.shape[1]
        row_wind = tuple(
            packed[layer_rows:].reshape(levels, 6, width_cells) for packed in shifted
        ) + (edge_speed,)
    above_wind, below_wind, edge_speed = row_wind
    above_layers, below_layers = (
        packed[:layer_rows].reshape(tracer.shape[0], tracer.shape[1], 6, 3, width_cells)
        for packed in shifted
    )
    at_top = position == band_count - 1
    at_bottom = position == 0
    padded_faces = []
    speed_faces = []
    for face_number in range(6):
        half = face_number // 2
        if face_number % 2 == 0:
            north_cells = jnp.where(
                at_top,
                jnp.flip(edge_layers[:, :, (half + 1) % 3], -1),
                above_layers[:, :, face_number],
            )
            north_speed = jnp.where(
                at_top,
                jnp.flip(edge_speed[:, (half + 1) % 3], -1),
                above_wind[:, face_number],
            )
            south_cells = jnp.where(
                at_bottom,
                below_layers[:, :, (face_number - 1) % 6],
                below_layers[:, :, face_number],
            )
            south_speed = jnp.where(
                at_bottom, below_wind[:, (face_number - 1) % 6], below_wind[:, face_number]
            )
        else:
            north_cells = jnp.where(
                at_top, above_layers[:, :, (face_number + 1) % 6], above_layers[:, :, face_number]
            )
            north_speed = jnp.where(
                at_top, above_wind[:, (face_number + 1) % 6], above_wind[:, face_number]
            )
            south_cells = jnp.where(
                at_bottom,
                jnp.flip(edge_layers[:, :, (half - 1) % 3], -1),
                below_layers[:, :, face_number],
            )
            south_speed = jnp.where(
                at_bottom,
                jnp.flip(edge_speed[:, (half - 1) % 3], -1),
                below_wind[:, face_number],
            )
        padded_faces.append(
            jnp.concatenate([south_cells, tracer[:, :, face_number], north_cells], -2)
        )
        speeds = jnp.concatenate(
            [south_speed[:, None, :], north_wind[:, face_number], north_speed[:, None, :]], -2
        )
        speed_faces.append(0.5 * (speeds[:, :-1, :] + speeds[:, 1:, :]))
    return (jnp.stack(padded_faces, 2), jnp.stack(speed_faces, 1), row_wind)


def regrid(tracer, tile_source, tile_target, intersection, band_count):
    scenarios = tracer.shape[0]
    levels = tracer.shape[1]
    batch_rows = scenarios * levels
    block_cells = intersection.shape[1]
    blocks = tracer.astype(jnp.bfloat16).reshape(batch_rows, -1, block_cells)
    chosen = jnp.take(blocks, tile_source, axis=1)
    partial_value = jnp.einsum(
        "btk,tkc->tbc", chosen, intersection, preferred_element_type=jnp.float32
    )
    target_band = tile_target // TGT_DEV
    target_block = tile_target % TGT_DEV
    band_hot = (target_band[:, None] == jnp.arange(band_count)[None, :]).astype(jnp.int32)
    rank = jnp.sum((jnp.cumsum(band_hot, 0) - band_hot) * band_hot, 1)
    slot = jnp.where(rank < SLOTS, target_band * SLOTS + rank, -1)
    slot_hot = (slot[None, :] == jnp.arange(band_count * SLOTS)[:, None]).astype(jnp.float32)
    slotted = jnp.einsum(
        "st,tbc->sbc", slot_hot, partial_value, precision=lax.Precision.HIGHEST
    )
    slot_block = jnp.sum(slot_hot * target_block[None, :].astype(jnp.float32), 1)
    index_rows = jnp.zeros((band_count, 8, block_cells), jnp.float32)
    index_rows = index_rows.at[:, 0, :SLOTS].set(slot_block.reshape(band_count, SLOTS))
    send = jnp.concatenate(
        [slotted.reshape(band_count, SLOTS * batch_rows, block_cells), index_rows], 1
    )
    got = lax.all_to_all(send, "space", 0, 0, tiled=True)
    values = got[:, : SLOTS * batch_rows].reshape(band_count * SLOTS, batch_rows, block_cells)
    got_block = got[:, SLOTS * batch_rows, :SLOTS].reshape(-1)
    block_hot = (got_block[None, :] == jnp.arange(TGT_DEV)[:, None].astype(jnp.float32)).astype(
        jnp.float32
    )
    summed = jnp.einsum("ks,sbc->bkc", block_hot, values, precision=lax.Precision.HIGHEST)
    return summed.reshape(scenarios, levels, TGT_DEV, block_cells)


def local(concentration, emissions, courant, tile_source, tile_target, intersection):
    band_count = lax.axis_size("space")
    position = lax.axis_index("space")
    tracer = concentration.at[:, 0].add(emissions)
    east_wind = courant[0]
    north_wind = courant[1]
    edge_wind = None
    row_wind = None
    for step_number in range(2):
        padded, courant_faces, edge_wind = column_halos(
            tracer, east_wind, north_wind, position, band_count, edge_wind
        )
        tracer = parabola_sweep(padded, courant_faces, 4)
        padded, courant_faces, row_wind = row_halos(
            tracer, east_wind, north_wind, position, band_count, row_wind
        )
        tracer = parabola_sweep(padded, courant_faces, 3)
    regridded = regrid(tracer, tile_source, tile_target, intersection, band_count)
    scenarios = tracer.shape[0]
    everyone = lax.all_gather(regridded, "scen", axis=0, tiled=True)
    moment_sums = jnp.stack([jnp.sum(everyone, 0), jnp.sum(everyone * everyone, 0)])
    ensemble_moments = moment_sums / (scenarios * lax.axis_size("scen"))
    return (tracer, regridded, ensemble_moments)


def solution(mesh):
    return jax.shard_map(
        local,
        mesh=mesh,
        in_specs=(
            P("scen", None, None, "space", None),
            P("scen", None, "space", None),
            P(None, None, None, "space", None),
            P("space"),
            P("space"),
            P("space", None, None),
        ),
        out_specs=(
            P("scen", None, None, "space", None),
            P("scen", None, "space", None),
            P(None, None, "space", None),
        ),
        check_vma=False,
    )
```

```python
import jax
import jax.numpy as jnp
from jax import lax
from jax.sharding import PartitionSpec as P

TGT_DEV = 32
SLOTS = 16


def from_behind(block, axis, distance):
    devices = range(lax.axis_size(axis))
    route = [((i - distance) % len(devices), i) for i in devices]
    return lax.ppermute(block, axis, route)


def parabola_sweep(padded, courant_faces, sweep_axis):
    cells_along = padded.shape[sweep_axis] - 6

    def window(values_in, first_cell, length):
        return lax.slice_in_dim(values_in, first_cell, first_cell + length, axis=sweep_axis)

    edge_values = 7.0 / 12.0 * (
        window(padded, 1, cells_along + 3) + window(padded, 2, cells_along + 3)
    ) - 1.0 / 12.0 * (window(padded, 0, cells_along + 3) + window(padded, 3, cells_along + 3))
    left_edge = window(edge_values, 0, cells_along + 2)
    right_edge = window(edge_values, 1, cells_along + 2)
    centre = window(padded, 2, cells_along + 2)
    slopes = right_edge - left_edge
    curvature = 6.0 * centre - 3.0 * (left_edge + right_edge)
    backward = -courant_faces
    upwind_left = courant_faces * (
        window(right_edge, 0, cells_along + 1)
        - 0.5
        * courant_faces
        * (
            window(slopes, 0, cells_along + 1)
            - (1.0 - 2.0 * courant_faces / 3.0) * window(curvature, 0, cells_along + 1)
        )
    )
    upwind_right = courant_faces * (
        window(left_edge, 1, cells_along + 1)
        + 0.5
        * backward
        * (
            window(slopes, 1, cells_along + 1)
            + (1.0 - 2.0 * backward / 3.0) * window(curvature, 1, cells_along + 1)
        )
    )
    fluxes = jnp.where(courant_faces >= 0.0, upwind_left, upwind_right)
    return window(padded, 3, cells_along) - (
        window(fluxes, 1, cells_along) - window(fluxes, 0, cells_along)
    )


def pack_rows(tracer, north_wind, lowest):
    row_count = tracer.shape[3]
    width_cells = tracer.shape[4]
    if lowest:
        layers = tracer[:, :, :, 0:3, :]
    else:
        layers = tracer[:, :, :, row_count - 3 :, :]
    parts = [layers.reshape(-1, width_cells)]
    if north_wind is not None:
        wind_row = north_wind[:, :, 0:1, :] if lowest else north_wind[:, :, row_count - 1 :, :]
        parts.append(wind_row.reshape(-1, width_cells))
    return jnp.concatenate(parts, 0)


def edge_rows(tracer, north_wind, position, band_count, with_wind):
    row_count = tracer.shape[3]
    width_cells = tracer.shape[4]
    top = [tracer[:, :, 0::2, row_count - 3 :, :].reshape(-1, width_cells)]
    low = [tracer[:, :, 1::2, 0:3, :].reshape(-1, width_cells)]
    if with_wind:
        top.append(north_wind[:, 0::2, row_count - 1, :].reshape(-1, width_cells))
        low.append(north_wind[:, 1::2, 0, :].reshape(-1, width_cells))
    top = jnp.concatenate(top, 0)
    low = jnp.concatenate(low, 0)
    send = jnp.where(position == band_count - 1, top, jnp.where(position == 0, low, 0.0))
    send = jnp.flip(send.T, 0).reshape(band_count, -1)
    got = lax.all_to_all(send, "space", 0, 0, tiled=True)
    count = top.shape[0]
    return got[band_count - 1].reshape(-1, count), got[0].reshape(-1, count)


def column_halos(tracer, east_wind, north_wind, position, band_count, edge_wind):
    scenarios, levels, _, row_count, width_cells = tracer.shape
    top, low = edge_rows(tracer, north_wind, position, band_count, edge_wind is None)
    cells = scenarios * levels * 3 * 3
    top_layers = top[:, :cells].reshape(row_count, scenarios, levels, 3, 3)
    low_layers = low[:, :cells].reshape(row_count, scenarios, levels, 3, 3)
    if edge_wind is None:
        edge_wind = (
            top[:, cells:].reshape(row_count, levels, 3),
            low[:, cells:].reshape(row_count, levels, 3),
        )
    top_wind, low_wind = edge_wind
    padded_faces = []
    speed_faces = []
    for face_number in range(6):
        half = face_number // 2
        if face_number % 2 == 0:
            west_cells = jnp.moveaxis(top_layers[:, :, :, (half - 1) % 3], 0, 2)
            west_speed = top_wind[:, :, (half - 1) % 3].T
            east_cells = tracer[:, :, (face_number + 1) % 6, :, 0:3]
            east_speed = east_wind[:, (face_number + 1) % 6, :, 0]
        else:
            west_cells = tracer[:, :, (face_number - 1) % 6, :, width_cells - 3 :]
            west_speed = east_wind[:, (face_number - 1) % 6, :, width_cells - 1]
            east_cells = jnp.moveaxis(low_layers[:, :, :, (half + 1) % 3], 0, 2)
            east_speed = low_wind[:, :, (half + 1) % 3].T
        padded_faces.append(
            jnp.concatenate([west_cells, tracer[:, :, face_number], east_cells], -1)
        )
        speeds = jnp.concatenate(
            [west_speed[:, :, None], east_wind[:, face_number], east_speed[:, :, None]], -1
        )
        speed_faces.append(0.5 * (speeds[:, :, :-1] + speeds[:, :, 1:]))
    return (jnp.stack(padded_faces, 2), jnp.stack(speed_faces, 1), edge_wind)


def edge_columns(tracer, east_wind, position, band_count, with_wind):
    scenarios, levels, _, row_count, width_cells = tracer.shape
    to_top = [jnp.moveaxis(tracer[:, :, 0::2, :, 0:3], 3, 0).reshape(row_count, -1)]
    to_low = [jnp.moveaxis(tracer[:, :, 1::2, :, width_cells - 3 :], 3, 0).reshape(row_count, -1)]
    if with_wind:
        to_top.append(jnp.moveaxis(east_wind[:, 0::2, :, 0], 2, 0).reshape(row_count, -1))
        to_low.append(
            jnp.moveaxis(east_wind[:, 1::2, :, width_cells - 1], 2, 0).reshape(row_count, -1)
        )
    to_top = jnp.concatenate(to_top, 1)
    to_low = jnp.concatenate(to_low, 1)
    count = to_top.shape[1]
    send = jnp.zeros((band_count, row_count, count), to_top.dtype)
    send = send.at[band_count - 1].set(to_top).at[0].set(to_low)
    got = lax.all_to_all(send, "space", 0, 0, tiled=True)
    flipped = jnp.flip(got.reshape(-1, count), 0).T
    cells = scenarios * levels * 3 * 3
    layers = flipped[:cells].reshape(scenarios, levels, 3, 3, band_count * row_count)
    wind = None
    if with_wind:
        wind = flipped[cells:].reshape(levels, 3, band_count * row_count)
    return layers, wind


def row_halos(tracer, east_wind, north_wind, position, band_count, row_wind):
    first_step = row_wind is None
    shifted = []
    for step_by, lowest in ((-1, True), (1, False)):
        packed = pack_rows(tracer, north_wind if first_step else None, lowest)
        shifted.append(from_behind(packed, "space", step_by))
    edge_layers, edge_speed = edge_columns(tracer, east_wind, position, band_count, first_step)
    layer_rows = tracer.shape[0] * tracer.shape[1] * 18
    width_cells = tracer.shape[4]
    if first_step:
        levels = tracer.shape[1]
        row_wind = tuple(
            packed[layer_rows:].reshape(levels, 6, width_cells) for packed in shifted
        ) + (edge_speed,)
    above_wind, below_wind, edge_speed = row_wind
    above_layers, below_layers = (
        packed[:layer_rows].reshape(tracer.shape[0], tracer.shape[1], 6, 3, width_cells)
        for packed in shifted
    )
    at_top = position == band_count - 1
    at_bottom = position == 0
    padded_faces = []
    speed_faces = []
    for face_number in range(6):
        half = face_number // 2
        if face_number % 2 == 0:
            north_cells = jnp.where(
                at_top,
                edge_layers[:, :, (half + 1) % 3],
                above_layers[:, :, face_number],
            )
            north_speed = jnp.where(
                at_top,
                edge_speed[:, (half + 1) % 3],
                above_wind[:, face_number],
            )
            south_cells = jnp.where(
                at_bottom,
                below_layers[:, :, (face_number - 1) % 6],
                below_layers[:, :, face_number],
            )
            south_speed = jnp.where(
                at_bottom, below_wind[:, (face_number - 1) % 6], below_wind[:, face_number]
            )
        else:
            north_cells = jnp.where(
                at_top, above_layers[:, :, (face_number + 1) % 6], above_layers[:, :, face_number]
            )
            north_speed = jnp.where(
                at_top, above_wind[:, (face_number + 1) % 6], above_wind[:, face_number]
            )
            south_cells = jnp.where(
                at_bottom,
                edge_layers[:, :, (half - 1) % 3],
                below_layers[:, :, face_number],
            )
            south_speed = jnp.where(
                at_bottom,
                edge_speed[:, (half - 1) % 3],
                below_wind[:, face_number],
            )
        padded_faces.append(
            jnp.concatenate([south_cells, tracer[:, :, face_number], north_cells], -2)
        )
        speeds = jnp.concatenate(
            [south_speed[:, None, :], north_wind[:, face_number], north_speed[:, None, :]], -2
        )
        speed_faces.append(0.5 * (speeds[:, :-1, :] + speeds[:, 1:, :]))
    return (jnp.stack(padded_faces, 2), jnp.stack(speed_faces, 1), row_wind)


def regrid(tracer, tile_source, tile_target, intersection, band_count):
    scenarios = tracer.shape[0]
    levels = tracer.shape[1]
    batch_rows = scenarios * levels
    block_cells = intersection.shape[1]
    blocks = tracer.astype(jnp.bfloat16).reshape(batch_rows, -1, block_cells)
    chosen = jnp.take(blocks, tile_source, axis=1)
    partial_value = jnp.einsum(
        "btk,tkc->tbc", chosen, intersection, preferred_element_type=jnp.float32
    )
    target_band = tile_target // TGT_DEV
    target_block = tile_target % TGT_DEV
    band_hot = (target_band[:, None] == jnp.arange(band_count)[None, :]).astype(jnp.int32)
    rank = jnp.sum((jnp.cumsum(band_hot, 0) - band_hot) * band_hot, 1)
    slot = jnp.where(rank < SLOTS, target_band * SLOTS + rank, -1)
    slot_hot = (slot[None, :] == jnp.arange(band_count * SLOTS)[:, None]).astype(jnp.float32)
    slotted = jnp.einsum(
        "st,tbc->sbc", slot_hot, partial_value, precision=lax.Precision.HIGHEST
    )
    slot_block = jnp.sum(slot_hot * target_block[None, :].astype(jnp.float32), 1)
    index_rows = jnp.zeros((band_count, 8, block_cells), jnp.float32)
    index_rows = index_rows.at[:, 0, :SLOTS].set(slot_block.reshape(band_count, SLOTS))
    send = jnp.concatenate(
        [slotted.reshape(band_count, SLOTS * batch_rows, block_cells), index_rows], 1
    )
    got = lax.all_to_all(send, "space", 0, 0, tiled=True)
    values = got[:, : SLOTS * batch_rows].reshape(band_count * SLOTS, batch_rows, block_cells)
    got_block = got[:, SLOTS * batch_rows, :SLOTS].reshape(-1)
    block_hot = (got_block[None, :] == jnp.arange(TGT_DEV)[:, None].astype(jnp.float32)).astype(
        jnp.float32
    )
    summed = jnp.einsum("ks,sbc->bkc", block_hot, values, precision=lax.Precision.HIGHEST)
    return summed.reshape(scenarios, levels, TGT_DEV, block_cells)


def local(concentration, emissions, courant, tile_source, tile_target, intersection):
    band_count = lax.axis_size("space")
    position = lax.axis_index("space")
    tracer = concentration.at[:, 0].add(emissions)
    east_wind = courant[0]
    north_wind = courant[1]
    edge_wind = None
    row_wind = None
    for step_number in range(2):
        padded, courant_faces, edge_wind = column_halos(
            tracer, east_wind, north_wind, position, band_count, edge_wind
        )
        tracer = parabola_sweep(padded, courant_faces, 4)
        padded, courant_faces, row_wind = row_halos(
            tracer, east_wind, north_wind, position, band_count, row_wind
        )
        tracer = parabola_sweep(padded, courant_faces, 3)
    regridded = regrid(tracer, tile_source, tile_target, intersection, band_count)
    scenarios = tracer.shape[0]
    scen_count = lax.axis_size("scen")
    copies = jnp.broadcast_to(regridded, (scen_count,) + regridded.shape[1:])
    everyone = lax.all_to_all(copies, "scen", 0, 0, tiled=True)
    moment_sums = jnp.stack([jnp.sum(everyone, 0), jnp.sum(everyone * everyone, 0)])
    ensemble_moments = moment_sums / (scenarios * lax.axis_size("scen"))
    return (tracer, regridded, ensemble_moments)


def solution(mesh):
    return jax.shard_map(
        local,
        mesh=mesh,
        in_specs=(
            P("scen", None, None, "space", None),
            P("scen", None, "space", None),
            P(None, None, None, "space", None),
            P("space"),
            P("space"),
            P("space", None, None),
        ),
        out_specs=(
            P("scen", None, None, "space", None),
            P("scen", None, "space", None),
            P(None, None, "space", None),
        ),
        check_vma=False,
    )
```

```python
import jax
import jax.numpy as jnp
from jax import lax
from jax.sharding import PartitionSpec as P

TGT_DEV = 32
SLOTS = 16


def from_behind(block, axis, distance):
    devices = range(lax.axis_size(axis))
    route = [((i - distance) % len(devices), i) for i in devices]
    return lax.ppermute(block, axis, route)


def parabola_sweep(padded, courant_faces, sweep_axis):
    cells_along = padded.shape[sweep_axis] - 6

    def window(values_in, first_cell, length):
        return lax.slice_in_dim(values_in, first_cell, first_cell + length, axis=sweep_axis)

    edge_values = 7.0 / 12.0 * (
        window(padded, 1, cells_along + 3) + window(padded, 2, cells_along + 3)
    ) - 1.0 / 12.0 * (window(padded, 0, cells_along + 3) + window(padded, 3, cells_along + 3))
    left_edge = window(edge_values, 0, cells_along + 2)
    right_edge = window(edge_values, 1, cells_along + 2)
    centre = window(padded, 2, cells_along + 2)
    slopes = right_edge - left_edge
    curvature = 6.0 * centre - 3.0 * (left_edge + right_edge)
    backward = -courant_faces
    upwind_left = courant_faces * (
        window(right_edge, 0, cells_along + 1)
        - 0.5
        * courant_faces
        * (
            window(slopes, 0, cells_along + 1)
            - (1.0 - 2.0 * courant_faces / 3.0) * window(curvature, 0, cells_along + 1)
        )
    )
    upwind_right = courant_faces * (
        window(left_edge, 1, cells_along + 1)
        + 0.5
        * backward
        * (
            window(slopes, 1, cells_along + 1)
            + (1.0 - 2.0 * backward / 3.0) * window(curvature, 1, cells_along + 1)
        )
    )
    fluxes = jnp.where(courant_faces >= 0.0, upwind_left, upwind_right)
    return window(padded, 3, cells_along) - (
        window(fluxes, 1, cells_along) - window(fluxes, 0, cells_along)
    )


def pack_rows(tracer, north_wind, lowest):
    row_count = tracer.shape[3]
    width_cells = tracer.shape[4]
    if lowest:
        layers = tracer[:, :, :, 0:3, :]
    else:
        layers = tracer[:, :, :, row_count - 3 :, :]
    parts = [layers.reshape(-1, width_cells)]
    if north_wind is not None:
        wind_row = north_wind[:, :, 0:1, :] if lowest else north_wind[:, :, row_count - 1 :, :]
        parts.append(wind_row.reshape(-1, width_cells))
    return jnp.concatenate(parts, 0)


def edge_rows(tracer, north_wind, position, band_count, with_wind):
    row_count = tracer.shape[3]
    width_cells = tracer.shape[4]
    top = [tracer[:, :, 0::2, row_count - 3 :, :].reshape(-1, width_cells)]
    low = [tracer[:, :, 1::2, 0:3, :].reshape(-1, width_cells)]
    if with_wind:
        top.append(north_wind[:, 0::2, row_count - 1, :].reshape(-1, width_cells))
        low.append(north_wind[:, 1::2, 0, :].reshape(-1, width_cells))
    top = jnp.concatenate(top, 0)
    low = jnp.concatenate(low, 0)
    send = jnp.where(position == band_count - 1, top, jnp.where(position == 0, low, 0.0))
    send = jnp.flip(send.T, 0).reshape(band_count, -1)
    got = lax.all_to_all(send, "space", 0, 0, tiled=True)
    count = top.shape[0]
    return got[band_count - 1].reshape(-1, count), got[0].reshape(-1, count)


def column_halos(tracer, east_wind, north_wind, position, band_count, edge_wind, faces_known):
    scenarios, levels, _, row_count, width_cells = tracer.shape
    top, low = edge_rows(tracer, north_wind, position, band_count, edge_wind is None)
    cells = scenarios * levels * 3 * 3
    top_layers = top[:, :cells].reshape(row_count, scenarios, levels, 3, 3)
    low_layers = low[:, :cells].reshape(row_count, scenarios, levels, 3, 3)
    if edge_wind is None:
        edge_wind = (
            top[:, cells:].reshape(row_count, levels, 3),
            low[:, cells:].reshape(row_count, levels, 3),
        )
    top_wind, low_wind = edge_wind
    west_faces, east_faces, west_speeds, east_speeds = [], [], [], []
    for face_number in range(6):
        half = face_number // 2
        if face_number % 2 == 0:
            west_cells = jnp.moveaxis(top_layers[:, :, :, (half - 1) % 3], 0, 2)
            west_speed = top_wind[:, :, (half - 1) % 3].T
            east_cells = tracer[:, :, (face_number + 1) % 6, :, 0:3]
            east_speed = east_wind[:, (face_number + 1) % 6, :, 0]
        else:
            west_cells = tracer[:, :, (face_number - 1) % 6, :, width_cells - 3 :]
            west_speed = east_wind[:, (face_number - 1) % 6, :, width_cells - 1]
            east_cells = jnp.moveaxis(low_layers[:, :, :, (half + 1) % 3], 0, 2)
            east_speed = low_wind[:, :, (half + 1) % 3].T
        west_faces.append(west_cells)
        east_faces.append(east_cells)
        west_speeds.append(west_speed)
        east_speeds.append(east_speed)
    padded = jnp.concatenate(
        [jnp.stack(west_faces, 2), tracer, jnp.stack(east_faces, 2)], -1
    )
    if faces_known is None:
        speeds = jnp.concatenate(
            [
                jnp.stack(west_speeds, 1)[..., None],
                east_wind,
                jnp.stack(east_speeds, 1)[..., None],
            ],
            -1,
        )
        faces_known = 0.5 * (speeds[..., :-1] + speeds[..., 1:])
    return (padded, faces_known, edge_wind)


def edge_columns(tracer, east_wind, position, band_count, with_wind):
    scenarios, levels, _, row_count, width_cells = tracer.shape
    to_top = [jnp.moveaxis(tracer[:, :, 0::2, :, 0:3], 3, 0).reshape(row_count, -1)]
    to_low = [jnp.moveaxis(tracer[:, :, 1::2, :, width_cells - 3 :], 3, 0).reshape(row_count, -1)]
    if with_wind:
        to_top.append(jnp.moveaxis(east_wind[:, 0::2, :, 0], 2, 0).reshape(row_count, -1))
        to_low.append(
            jnp.moveaxis(east_wind[:, 1::2, :, width_cells - 1], 2, 0).reshape(row_count, -1)
        )
    to_top = jnp.concatenate(to_top, 1)
    to_low = jnp.concatenate(to_low, 1)
    count = to_top.shape[1]
    send = jnp.zeros((band_count, row_count, count), to_top.dtype)
    send = send.at[band_count - 1].set(to_top).at[0].set(to_low)
    got = lax.all_to_all(send, "space", 0, 0, tiled=True)
    flipped = jnp.flip(got.reshape(-1, count), 0).T
    cells = scenarios * levels * 3 * 3
    layers = flipped[:cells].reshape(scenarios, levels, 3, 3, band_count * row_count)
    wind = None
    if with_wind:
        wind = flipped[cells:].reshape(levels, 3, band_count * row_count)
    return layers, wind


def row_halos(tracer, east_wind, north_wind, position, band_count, row_wind, faces_known):
    first_step = row_wind is None
    shifted = []
    for step_by, lowest in ((-1, True), (1, False)):
        packed = pack_rows(tracer, north_wind if first_step else None, lowest)
        shifted.append(from_behind(packed, "space", step_by))
    edge_layers, edge_speed = edge_columns(tracer, east_wind, position, band_count, first_step)
    layer_rows = tracer.shape[0] * tracer.shape[1] * 18
    width_cells = tracer.shape[4]
    if first_step:
        levels = tracer.shape[1]
        row_wind = tuple(
            packed[layer_rows:].reshape(levels, 6, width_cells) for packed in shifted
        ) + (edge_speed,)
    above_wind, below_wind, edge_speed = row_wind
    above_layers, below_layers = (
        packed[:layer_rows].reshape(tracer.shape[0], tracer.shape[1], 6, 3, width_cells)
        for packed in shifted
    )
    at_top = position == band_count - 1
    at_bottom = position == 0
    south_faces, north_faces, south_speeds, north_speeds = [], [], [], []
    for face_number in range(6):
        half = face_number // 2
        if face_number % 2 == 0:
            north_cells = jnp.where(
                at_top,
                edge_layers[:, :, (half + 1) % 3],
                above_layers[:, :, face_number],
            )
            north_speed = jnp.where(
                at_top,
                edge_speed[:, (half + 1) % 3],
                above_wind[:, face_number],
            )
            south_cells = jnp.where(
                at_bottom,
                below_layers[:, :, (face_number - 1) % 6],
                below_layers[:, :, face_number],
            )
            south_speed = jnp.where(
                at_bottom, below_wind[:, (face_number - 1) % 6], below_wind[:, face_number]
            )
        else:
            north_cells = jnp.where(
                at_top, above_layers[:, :, (face_number + 1) % 6], above_layers[:, :, face_number]
            )
            north_speed = jnp.where(
                at_top, above_wind[:, (face_number + 1) % 6], above_wind[:, face_number]
            )
            south_cells = jnp.where(
                at_bottom,
                edge_layers[:, :, (half - 1) % 3],
                below_layers[:, :, face_number],
            )
            south_speed = jnp.where(
                at_bottom,
                edge_speed[:, (half - 1) % 3],
                below_wind[:, face_number],
            )
        south_faces.append(south_cells)
        north_faces.append(north_cells)
        south_speeds.append(south_speed)
        north_speeds.append(north_speed)
    padded = jnp.concatenate(
        [jnp.stack(south_faces, 2), tracer, jnp.stack(north_faces, 2)], -2
    )
    if faces_known is None:
        speeds = jnp.concatenate(
            [
                jnp.stack(south_speeds, 1)[:, :, None, :],
                north_wind,
                jnp.stack(north_speeds, 1)[:, :, None, :],
            ],
            -2,
        )
        faces_known = 0.5 * (speeds[:, :, :-1, :] + speeds[:, :, 1:, :])
    return (padded, faces_known, row_wind)


def regrid(tracer, tile_source, tile_target, intersection, band_count):
    scenarios = tracer.shape[0]
    levels = tracer.shape[1]
    batch_rows = scenarios * levels
    block_cells = intersection.shape[1]
    blocks = tracer.astype(jnp.bfloat16).reshape(batch_rows, -1, block_cells)
    chosen = jnp.take(blocks, tile_source, axis=1)
    partial_value = jnp.einsum(
        "btk,tkc->tbc", chosen, intersection, preferred_element_type=jnp.float32
    )
    target_band = tile_target // TGT_DEV
    target_block = tile_target % TGT_DEV
    band_hot = (target_band[:, None] == jnp.arange(band_count)[None, :]).astype(jnp.int32)
    rank = jnp.sum((jnp.cumsum(band_hot, 0) - band_hot) * band_hot, 1)
    slot = jnp.where(rank < SLOTS, target_band * SLOTS + rank, -1)
    slot_hot = (slot[None, :] == jnp.arange(band_count * SLOTS)[:, None]).astype(jnp.float32)
    slotted = jnp.einsum(
        "st,tbc->sbc", slot_hot, partial_value, precision=lax.Precision.HIGHEST
    )
    slot_block = jnp.sum(slot_hot * target_block[None, :].astype(jnp.float32), 1)
    index_rows = jnp.zeros((band_count, 8, block_cells), jnp.float32)
    index_rows = index_rows.at[:, 0, :SLOTS].set(slot_block.reshape(band_count, SLOTS))
    send = jnp.concatenate(
        [slotted.reshape(band_count, SLOTS * batch_rows, block_cells), index_rows], 1
    )
    got = lax.all_to_all(send, "space", 0, 0, tiled=True)
    values = got[:, : SLOTS * batch_rows].reshape(band_count * SLOTS, batch_rows, block_cells)
    got_block = got[:, SLOTS * batch_rows, :SLOTS].reshape(-1)
    block_hot = (got_block[None, :] == jnp.arange(TGT_DEV)[:, None].astype(jnp.float32)).astype(
        jnp.float32
    )
    summed = jnp.einsum("ks,sbc->bkc", block_hot, values, precision=lax.Precision.HIGHEST)
    return summed.reshape(scenarios, levels, TGT_DEV, block_cells)


def moments_of(regridded):
    scenarios = regridded.shape[0]
    scen_count = lax.axis_size("scen")
    copies = jnp.broadcast_to(regridded, (scen_count,) + regridded.shape[1:])
    everyone = lax.all_to_all(copies, "scen", 0, 0, tiled=True)
    moment_sums = jnp.stack([jnp.sum(everyone, 0), jnp.sum(everyone * everyone, 0)])
    return moment_sums / (scenarios * scen_count)


def local(concentration, emissions, courant, tile_source, tile_target, intersection):
    band_count = lax.axis_size("space")
    position = lax.axis_index("space")
    tracer = concentration.at[:, 0].add(emissions)
    east_wind = courant[0]
    north_wind = courant[1]
    edge_wind = None
    row_wind = None
    cx = None
    cy = None
    for step_number in range(2):
        padded, cx, edge_wind = column_halos(
            tracer, east_wind, north_wind, position, band_count, edge_wind, cx
        )
        tracer = parabola_sweep(padded, cx, 4)
        padded, cy, row_wind = row_halos(
            tracer, east_wind, north_wind, position, band_count, row_wind, cy
        )
        tracer = parabola_sweep(padded, cy, 3)
    regridded = regrid(tracer, tile_source, tile_target, intersection, band_count)
    ensemble_moments = moments_of(regridded)
    return (tracer, regridded, ensemble_moments)


def solution(mesh):
    return jax.shard_map(
        local,
        mesh=mesh,
        in_specs=(
            P("scen", None, None, "space", None),
            P("scen", None, "space", None),
            P(None, None, None, "space", None),
            P("space"),
            P("space"),
            P("space", None, None),
        ),
        out_specs=(
            P("scen", None, None, "space", None),
            P("scen", None, "space", None),
            P(None, None, "space", None),
        ),
        check_vma=False,
    )
```

```python
import jax
import jax.numpy as jnp
from jax import lax
from jax.sharding import PartitionSpec as P

TGT_DEV = 32
SLOTS = 16


def from_behind(block, axis, distance):
    devices = range(lax.axis_size(axis))
    route = [((i - distance) % len(devices), i) for i in devices]
    return lax.ppermute(block, axis, route)


def parabola_sweep(padded, courant_faces, sweep_axis):
    cells_along = padded.shape[sweep_axis] - 6

    def window(values_in, first_cell, length):
        return lax.slice_in_dim(values_in, first_cell, first_cell + length, axis=sweep_axis)

    edge_values = 7.0 / 12.0 * (
        window(padded, 1, cells_along + 3) + window(padded, 2, cells_along + 3)
    ) - 1.0 / 12.0 * (window(padded, 0, cells_along + 3) + window(padded, 3, cells_along + 3))
    left_edge = window(edge_values, 0, cells_along + 2)
    right_edge = window(edge_values, 1, cells_along + 2)
    centre = window(padded, 2, cells_along + 2)
    slopes = right_edge - left_edge
    curvature = 6.0 * centre - 3.0 * (left_edge + right_edge)
    backward = -courant_faces
    upwind_left = courant_faces * (
        window(right_edge, 0, cells_along + 1)
        - 0.5
        * courant_faces
        * (
            window(slopes, 0, cells_along + 1)
            - (1.0 - 2.0 * courant_faces / 3.0) * window(curvature, 0, cells_along + 1)
        )
    )
    upwind_right = courant_faces * (
        window(left_edge, 1, cells_along + 1)
        + 0.5
        * backward
        * (
            window(slopes, 1, cells_along + 1)
            + (1.0 - 2.0 * backward / 3.0) * window(curvature, 1, cells_along + 1)
        )
    )
    fluxes = jnp.where(courant_faces >= 0.0, upwind_left, upwind_right)
    return window(padded, 3, cells_along) - (
        window(fluxes, 1, cells_along) - window(fluxes, 0, cells_along)
    )


def pack_rows(tracer, north_wind, lowest):
    row_count = tracer.shape[3]
    width_cells = tracer.shape[4]
    if lowest:
        layers = tracer[:, :, :, 0:3, :]
    else:
        layers = tracer[:, :, :, row_count - 3 :, :]
    parts = [layers.reshape(-1, width_cells)]
    if north_wind is not None:
        wind_row = north_wind[:, :, 0:1, :] if lowest else north_wind[:, :, row_count - 1 :, :]
        parts.append(wind_row.reshape(-1, width_cells))
    return jnp.concatenate(parts, 0)


def edge_rows(tracer, north_wind, east_wind, position, band_count, with_wind):
    levels = tracer.shape[1]
    row_count = tracer.shape[3]
    width_cells = tracer.shape[4]
    column_wind = (
        jnp.moveaxis(east_wind[:, 0::2, :, 0], 2, 0).reshape(row_count, -1),
        jnp.moveaxis(east_wind[:, 1::2, :, width_cells - 1], 2, 0).reshape(row_count, -1),
    )
    top = [tracer[:, :, 0::2, row_count - 3 :, :].reshape(-1, width_cells)]
    low = [tracer[:, :, 1::2, 0:3, :].reshape(-1, width_cells)]
    if with_wind:
        top.append(north_wind[:, 0::2, row_count - 1, :].reshape(-1, width_cells))
        low.append(north_wind[:, 1::2, 0, :].reshape(-1, width_cells))
    top = jnp.concatenate(top, 0)
    low = jnp.concatenate(low, 0)
    send = jnp.where(position == band_count - 1, top, jnp.where(position == 0, low, 0.0))
    count = top.shape[0]
    send = jnp.flip(send.T, 0).reshape(band_count, row_count, count)
    if with_wind:
        gathered = jnp.zeros((band_count,) + column_wind[0].shape, send.dtype)
        gathered = gathered.at[band_count - 1].set(column_wind[0]).at[0].set(column_wind[1])
        send = jnp.concatenate([send, gathered], 2)
    got = lax.all_to_all(send, "space", 0, 0, tiled=True)
    wind = None
    if with_wind:
        extra = got[:, :, count:].reshape(band_count * row_count, -1)
        wind = jnp.flip(extra, 0).T.reshape(levels, 3, band_count * row_count)
    return got[band_count - 1, :, :count], got[0, :, :count], wind


def column_halos(tracer, east_wind, north_wind, position, band_count, edge_wind, faces_known):
    scenarios, levels, _, row_count, width_cells = tracer.shape
    top, low, column_wind = edge_rows(
        tracer, north_wind, east_wind, position, band_count, edge_wind is None
    )
    cells = scenarios * levels * 3 * 3
    top_layers = top[:, :cells].reshape(row_count, scenarios, levels, 3, 3)
    low_layers = low[:, :cells].reshape(row_count, scenarios, levels, 3, 3)
    if edge_wind is None:
        edge_wind = (
            top[:, cells:].reshape(row_count, levels, 3),
            low[:, cells:].reshape(row_count, levels, 3),
            column_wind,
        )
    top_wind, low_wind, _ = edge_wind
    west_faces, east_faces, west_speeds, east_speeds = [], [], [], []
    for face_number in range(6):
        half = face_number // 2
        if face_number % 2 == 0:
            west_cells = jnp.moveaxis(top_layers[:, :, :, (half - 1) % 3], 0, 2)
            west_speed = top_wind[:, :, (half - 1) % 3].T
            east_cells = tracer[:, :, (face_number + 1) % 6, :, 0:3]
            east_speed = east_wind[:, (face_number + 1) % 6, :, 0]
        else:
            west_cells = tracer[:, :, (face_number - 1) % 6, :, width_cells - 3 :]
            west_speed = east_wind[:, (face_number - 1) % 6, :, width_cells - 1]
            east_cells = jnp.moveaxis(low_layers[:, :, :, (half + 1) % 3], 0, 2)
            east_speed = low_wind[:, :, (half + 1) % 3].T
        west_faces.append(west_cells)
        east_faces.append(east_cells)
        west_speeds.append(west_speed)
        east_speeds.append(east_speed)
    padded = jnp.concatenate(
        [jnp.stack(west_faces, 2), tracer, jnp.stack(east_faces, 2)], -1
    )
    if faces_known is None:
        speeds = jnp.concatenate(
            [
                jnp.stack(west_speeds, 1)[..., None],
                east_wind,
                jnp.stack(east_speeds, 1)[..., None],
            ],
            -1,
        )
        faces_known = 0.5 * (speeds[..., :-1] + speeds[..., 1:])
    return (padded, faces_known, edge_wind)


def edge_columns(tracer, east_wind, position, band_count, with_wind):
    scenarios, levels, _, row_count, width_cells = tracer.shape
    to_top = [jnp.moveaxis(tracer[:, :, 0::2, :, 0:3], 3, 0).reshape(row_count, -1)]
    to_low = [jnp.moveaxis(tracer[:, :, 1::2, :, width_cells - 3 :], 3, 0).reshape(row_count, -1)]
    if with_wind:
        to_top.append(jnp.moveaxis(east_wind[:, 0::2, :, 0], 2, 0).reshape(row_count, -1))
        to_low.append(
            jnp.moveaxis(east_wind[:, 1::2, :, width_cells - 1], 2, 0).reshape(row_count, -1)
        )
    to_top = jnp.concatenate(to_top, 1)
    to_low = jnp.concatenate(to_low, 1)
    count = to_top.shape[1]
    send = jnp.zeros((band_count, row_count, count), to_top.dtype)
    send = send.at[band_count - 1].set(to_top).at[0].set(to_low)
    got = lax.all_to_all(send, "space", 0, 0, tiled=True)
    flipped = jnp.flip(got.reshape(-1, count), 0).T
    cells = scenarios * levels * 3 * 3
    layers = flipped[:cells].reshape(scenarios, levels, 3, 3, band_count * row_count)
    wind = None
    if with_wind:
        wind = flipped[cells:].reshape(levels, 3, band_count * row_count)
    return layers, wind


def row_halos(tracer, east_wind, north_wind, position, band_count, row_wind, faces_known):
    shifted = []
    for step_by, lowest in ((-1, True), (1, False)):
        packed = pack_rows(tracer, None, lowest)
        shifted.append(from_behind(packed, "space", step_by))
    edge_layers, _ = edge_columns(tracer, east_wind, position, band_count, False)
    layer_rows = tracer.shape[0] * tracer.shape[1] * 18
    width_cells = tracer.shape[4]
    above_wind, below_wind, edge_speed = row_wind
    above_layers, below_layers = (
        packed[:layer_rows].reshape(tracer.shape[0], tracer.shape[1], 6, 3, width_cells)
        for packed in shifted
    )
    at_top = position == band_count - 1
    at_bottom = position == 0
    south_faces, north_faces, south_speeds, north_speeds = [], [], [], []
    for face_number in range(6):
        half = face_number // 2
        if face_number % 2 == 0:
            north_cells = jnp.where(
                at_top,
                edge_layers[:, :, (half + 1) % 3],
                above_layers[:, :, face_number],
            )
            north_speed = jnp.where(
                at_top,
                edge_speed[:, (half + 1) % 3],
                above_wind[:, face_number],
            )
            south_cells = jnp.where(
                at_bottom,
                below_layers[:, :, (face_number - 1) % 6],
                below_layers[:, :, face_number],
            )
            south_speed = jnp.where(
                at_bottom, below_wind[:, (face_number - 1) % 6], below_wind[:, face_number]
            )
        else:
            north_cells = jnp.where(
                at_top, above_layers[:, :, (face_number + 1) % 6], above_layers[:, :, face_number]
            )
            north_speed = jnp.where(
                at_top, above_wind[:, (face_number + 1) % 6], above_wind[:, face_number]
            )
            south_cells = jnp.where(
                at_bottom,
                edge_layers[:, :, (half - 1) % 3],
                below_layers[:, :, face_number],
            )
            south_speed = jnp.where(
                at_bottom,
                edge_speed[:, (half - 1) % 3],
                below_wind[:, face_number],
            )
        south_faces.append(south_cells)
        north_faces.append(north_cells)
        south_speeds.append(south_speed)
        north_speeds.append(north_speed)
    padded = jnp.concatenate(
        [jnp.stack(south_faces, 2), tracer, jnp.stack(north_faces, 2)], -2
    )
    if faces_known is None:
        speeds = jnp.concatenate(
            [
                jnp.stack(south_speeds, 1)[:, :, None, :],
                north_wind,
                jnp.stack(north_speeds, 1)[:, :, None, :],
            ],
            -2,
        )
        faces_known = 0.5 * (speeds[:, :, :-1, :] + speeds[:, :, 1:, :])
    return (padded, faces_known, row_wind)


def regrid(tracer, tile_source, tile_target, intersection, band_count):
    scenarios = tracer.shape[0]
    levels = tracer.shape[1]
    batch_rows = scenarios * levels
    block_cells = intersection.shape[1]
    blocks = tracer.astype(jnp.bfloat16).reshape(batch_rows, -1, block_cells)
    chosen = jnp.take(blocks, tile_source, axis=1)
    partial_value = jnp.einsum(
        "btk,tkc->tbc", chosen, intersection, preferred_element_type=jnp.float32
    )
    target_band = tile_target // TGT_DEV
    target_block = tile_target % TGT_DEV
    band_hot = (target_band[:, None] == jnp.arange(band_count)[None, :]).astype(jnp.int32)
    rank = jnp.sum((jnp.cumsum(band_hot, 0) - band_hot) * band_hot, 1)
    slot = jnp.where(rank < SLOTS, target_band * SLOTS + rank, -1)
    slot_hot = (slot[None, :] == jnp.arange(band_count * SLOTS)[:, None]).astype(jnp.float32)
    slotted = jnp.einsum(
        "st,tbc->sbc", slot_hot, partial_value, precision=lax.Precision.HIGHEST
    )
    slot_block = jnp.sum(slot_hot * target_block[None, :].astype(jnp.float32), 1)
    index_rows = jnp.zeros((band_count, 8, block_cells), jnp.float32)
    index_rows = index_rows.at[:, 0, :SLOTS].set(slot_block.reshape(band_count, SLOTS))
    send = jnp.concatenate(
        [slotted.reshape(band_count, SLOTS * batch_rows, block_cells), index_rows], 1
    )
    got = lax.all_to_all(send, "space", 0, 0, tiled=True)
    values = got[:, : SLOTS * batch_rows].reshape(band_count * SLOTS, batch_rows, block_cells)
    got_block = got[:, SLOTS * batch_rows, :SLOTS].reshape(-1)
    block_hot = (got_block[None, :] == jnp.arange(TGT_DEV)[:, None].astype(jnp.float32)).astype(
        jnp.float32
    )
    summed = jnp.einsum("ks,sbc->bkc", block_hot, values, precision=lax.Precision.HIGHEST)
    return summed.reshape(scenarios, levels, TGT_DEV, block_cells)


def moments_of(regridded):
    scenarios = regridded.shape[0]
    scen_count = lax.axis_size("scen")
    copies = jnp.broadcast_to(regridded, (scen_count,) + regridded.shape[1:])
    everyone = lax.all_to_all(copies, "scen", 0, 0, tiled=True)
    moment_sums = jnp.stack([jnp.sum(everyone, 0), jnp.sum(everyone * everyone, 0)])
    return moment_sums / (scenarios * scen_count)


def local(concentration, emissions, courant, tile_source, tile_target, intersection):
    band_count = lax.axis_size("space")
    position = lax.axis_index("space")
    tracer = concentration.at[:, 0].add(emissions)
    east_wind = courant[0]
    north_wind = courant[1]
    edge_wind = None
    row_count = tracer.shape[3]
    row_wind = None
    neighbour_wind = (
        from_behind(north_wind[:, :, 0, :], "space", -1),
        from_behind(north_wind[:, :, row_count - 1, :], "space", 1),
    )
    cx = None
    cy = None
    for step_number in range(2):
        padded, cx, edge_wind = column_halos(
            tracer, east_wind, north_wind, position, band_count, edge_wind, cx
        )
        tracer = parabola_sweep(padded, cx, 4)
        row_wind = neighbour_wind + (edge_wind[2],)
        padded, cy, row_wind = row_halos(
            tracer, east_wind, north_wind, position, band_count, row_wind, cy
        )
        tracer = parabola_sweep(padded, cy, 3)
    regridded = regrid(tracer, tile_source, tile_target, intersection, band_count)
    ensemble_moments = moments_of(regridded)
    return (tracer, regridded, ensemble_moments)


def solution(mesh):
    return jax.shard_map(
        local,
        mesh=mesh,
        in_specs=(
            P("scen", None, None, "space", None),
            P("scen", None, "space", None),
            P(None, None, None, "space", None),
            P("space"),
            P("space"),
            P("space", None, None),
        ),
        out_specs=(
            P("scen", None, None, "space", None),
            P("scen", None, "space", None),
            P(None, None, "space", None),
        ),
        check_vma=False,
    )
```

```python
import jax
import jax.numpy as jnp
from jax import lax
from jax.sharding import PartitionSpec as P

TGT_DEV = 32
SLOTS = 16


def from_behind(block, axis, distance):
    devices = range(lax.axis_size(axis))
    route = [((i - distance) % len(devices), i) for i in devices]
    return lax.ppermute(block, axis, route)


def parabola_sweep(padded, courant_faces, sweep_axis):
    cells_along = padded.shape[sweep_axis] - 6

    def window(values_in, first_cell, length):
        return lax.slice_in_dim(values_in, first_cell, first_cell + length, axis=sweep_axis)

    edge_values = 7.0 / 12.0 * (
        window(padded, 1, cells_along + 3) + window(padded, 2, cells_along + 3)
    ) - 1.0 / 12.0 * (window(padded, 0, cells_along + 3) + window(padded, 3, cells_along + 3))
    left_edge = window(edge_values, 0, cells_along + 2)
    right_edge = window(edge_values, 1, cells_along + 2)
    centre = window(padded, 2, cells_along + 2)
    slopes = right_edge - left_edge
    curvature = 6.0 * centre - 3.0 * (left_edge + right_edge)
    backward = -courant_faces
    upwind_left = courant_faces * (
        window(right_edge, 0, cells_along + 1)
        - 0.5
        * courant_faces
        * (
            window(slopes, 0, cells_along + 1)
            - (1.0 - 2.0 * courant_faces / 3.0) * window(curvature, 0, cells_along + 1)
        )
    )
    upwind_right = courant_faces * (
        window(left_edge, 1, cells_along + 1)
        + 0.5
        * backward
        * (
            window(slopes, 1, cells_along + 1)
            + (1.0 - 2.0 * backward / 3.0) * window(curvature, 1, cells_along + 1)
        )
    )
    fluxes = jnp.where(courant_faces >= 0.0, upwind_left, upwind_right)
    return window(padded, 3, cells_along) - (
        window(fluxes, 1, cells_along) - window(fluxes, 0, cells_along)
    )


def pack_rows(tracer, north_wind, lowest):
    row_count = tracer.shape[3]
    width_cells = tracer.shape[4]
    if lowest:
        layers = tracer[:, :, :, 0:3, :]
    else:
        layers = tracer[:, :, :, row_count - 3 :, :]
    parts = [layers.reshape(-1, width_cells)]
    if north_wind is not None:
        wind_row = north_wind[:, :, 0:1, :] if lowest else north_wind[:, :, row_count - 1 :, :]
        parts.append(wind_row.reshape(-1, width_cells))
    return jnp.concatenate(parts, 0)


def first_exchange(tracer, north_wind, position, band_count):
    scenarios, levels, _, row_count, width_cells = tracer.shape
    top = jnp.concatenate(
        [
            tracer[:, :, 0::2, row_count - 3 :, :].reshape(-1, width_cells),
            north_wind[:, 0::2, row_count - 4 :, :].reshape(-1, width_cells),
        ],
        0,
    )
    low = jnp.concatenate(
        [
            tracer[:, :, 1::2, 0:3, :].reshape(-1, width_cells),
            north_wind[:, 1::2, 0:4, :].reshape(-1, width_cells),
        ],
        0,
    )
    send = jnp.where(position == band_count - 1, top, jnp.where(position == 0, low, 0.0))
    send = jnp.flip(send.T, 0).reshape(band_count, -1)
    got = lax.all_to_all(send, "space", 0, 0, tiled=True)
    count = top.shape[0]
    cells = scenarios * levels * 3 * 3

    def cells_of(block):
        return jnp.moveaxis(block[:, :cells].reshape(row_count, scenarios, levels, 3, 3), 0, 3)

    def wind_of(block):
        return jnp.moveaxis(block[:, cells:].reshape(row_count, levels, 3, 4), 0, 2)

    top_got = got[band_count - 1].reshape(row_count, count)
    low_got = got[0].reshape(row_count, count)
    return cells_of(top_got), cells_of(low_got), wind_of(top_got), wind_of(low_got)


def next_edge_cells(swept, east_wind, rows_top, rows_low, top_wind, low_wind):
    width_cells = swept.shape[4]
    halo_top = jnp.stack([swept[:, :, (2 * e + 2) % 6, :, 0:3] for e in range(3)], 2)
    halo_low = jnp.stack([swept[:, :, (2 * o - 1) % 6, :, width_cells - 3 :] for o in range(3)], 2)
    speed_top = jnp.stack([east_wind[:, (2 * e + 2) % 6, :, 0] for e in range(3)], 1)
    speed_low = jnp.stack([east_wind[:, (2 * o - 1) % 6, :, width_cells - 1] for o in range(3)], 1)
    speeds_top = jnp.concatenate([top_wind, speed_top[..., None]], -1)
    speeds_low = jnp.concatenate([speed_low[..., None], low_wind], -1)
    faces_top = 0.5 * (speeds_top[..., :-1] + speeds_top[..., 1:])
    faces_low = 0.5 * (speeds_low[..., :-1] + speeds_low[..., 1:])
    top_cells = parabola_sweep(jnp.concatenate([rows_top, halo_top], -1), faces_top, 4)
    low_cells = parabola_sweep(jnp.concatenate([halo_low, rows_low], -1), faces_low, 4)
    return top_cells, low_cells


def column_halos(tracer, east_wind, top_cells, low_cells, top_wind, low_wind, faces_known):
    width_cells = tracer.shape[4]
    west_faces, east_faces, west_speeds, east_speeds = [], [], [], []
    for face_number in range(6):
        half = face_number // 2
        if face_number % 2 == 0:
            west_cells = top_cells[:, :, (half - 1) % 3]
            west_speed = top_wind[:, (half - 1) % 3, :, 3]
            east_cells = tracer[:, :, (face_number + 1) % 6, :, 0:3]
            east_speed = east_wind[:, (face_number + 1) % 6, :, 0]
        else:
            west_cells = tracer[:, :, (face_number - 1) % 6, :, width_cells - 3 :]
            west_speed = east_wind[:, (face_number - 1) % 6, :, width_cells - 1]
            east_cells = low_cells[:, :, (half + 1) % 3]
            east_speed = low_wind[:, (half + 1) % 3, :, 0]
        west_faces.append(west_cells)
        east_faces.append(east_cells)
        west_speeds.append(west_speed)
        east_speeds.append(east_speed)
    padded = jnp.concatenate(
        [jnp.stack(west_faces, 2), tracer, jnp.stack(east_faces, 2)], -1
    )
    if faces_known is None:
        speeds = jnp.concatenate(
            [
                jnp.stack(west_speeds, 1)[..., None],
                east_wind,
                jnp.stack(east_speeds, 1)[..., None],
            ],
            -1,
        )
        faces_known = 0.5 * (speeds[..., :-1] + speeds[..., 1:])
    return padded, faces_known


def edge_columns(tracer, east_wind, position, band_count, with_wind, scatter_rows):
    scenarios, levels, _, row_count, width_cells = tracer.shape
    to_top = [jnp.moveaxis(tracer[:, :, 0::2, :, 0:3], 3, 0).reshape(row_count, -1)]
    to_low = [jnp.moveaxis(tracer[:, :, 1::2, :, width_cells - 3 :], 3, 0).reshape(row_count, -1)]
    if with_wind:
        to_top.append(jnp.moveaxis(east_wind[:, 0::2, :, 0], 2, 0).reshape(row_count, -1))
        to_low.append(
            jnp.moveaxis(east_wind[:, 1::2, :, width_cells - 1], 2, 0).reshape(row_count, -1)
        )
    to_top = jnp.concatenate(to_top, 1)
    to_low = jnp.concatenate(to_low, 1)
    count = to_top.shape[1]
    send = jnp.zeros((band_count, row_count, count), to_top.dtype)
    send = send.at[band_count - 1].set(to_top).at[0].set(to_low)
    if scatter_rows:
        rows_top = tracer[:, :, 0::2, row_count - 6 :, :].reshape(-1, width_cells)
        rows_low = tracer[:, :, 1::2, 0:6, :].reshape(-1, width_cells)
        chosen = jnp.where(
            position == band_count - 1, rows_top, jnp.where(position == 0, rows_low, 0.0)
        )
        scattered = jnp.flip(chosen.T, 0).reshape(band_count, row_count, rows_top.shape[0])
        send = jnp.concatenate([send, scattered], 2)
    got = lax.all_to_all(send, "space", 0, 0, tiled=True)
    extra = None
    if scatter_rows:

        def rows_of(block):
            return jnp.moveaxis(block.reshape(row_count, scenarios, levels, 3, 6), 0, 3)

        extra = (rows_of(got[band_count - 1, :, count:]), rows_of(got[0, :, count:]))
        got = got[:, :, :count]
    flipped = jnp.flip(got.reshape(-1, count), 0).T
    cells = scenarios * levels * 3 * 3
    layers = flipped[:cells].reshape(scenarios, levels, 3, 3, band_count * row_count)
    wind = None
    if with_wind:
        wind = flipped[cells:].reshape(levels, 3, band_count * row_count)
    return layers, wind, extra


def row_halos(
    tracer, east_wind, north_wind, position, band_count, row_wind, faces_known, scatter_rows
):
    first_step = row_wind is None
    shifted = []
    for step_by, lowest in ((-1, True), (1, False)):
        packed = pack_rows(tracer, north_wind if first_step else None, lowest)
        shifted.append(from_behind(packed, "space", step_by))
    edge_layers, edge_speed, extra = edge_columns(
        tracer, east_wind, position, band_count, first_step, scatter_rows
    )
    layer_rows = tracer.shape[0] * tracer.shape[1] * 18
    width_cells = tracer.shape[4]
    if first_step:
        levels = tracer.shape[1]
        row_wind = tuple(
            packed[layer_rows:].reshape(levels, 6, width_cells) for packed in shifted
        ) + (edge_speed,)
    above_wind, below_wind, edge_speed = row_wind
    above_layers, below_layers = (
        packed[:layer_rows].reshape(tracer.shape[0], tracer.shape[1], 6, 3, width_cells)
        for packed in shifted
    )
    at_top = position == band_count - 1
    at_bottom = position == 0
    south_faces, north_faces, south_speeds, north_speeds = [], [], [], []
    for face_number in range(6):
        half = face_number // 2
        if face_number % 2 == 0:
            north_cells = jnp.where(
                at_top,
                edge_layers[:, :, (half + 1) % 3],
                above_layers[:, :, face_number],
            )
            north_speed = jnp.where(
                at_top,
                edge_speed[:, (half + 1) % 3],
                above_wind[:, face_number],
            )
            south_cells = jnp.where(
                at_bottom,
                below_layers[:, :, (face_number - 1) % 6],
                below_layers[:, :, face_number],
            )
            south_speed = jnp.where(
                at_bottom, below_wind[:, (face_number - 1) % 6], below_wind[:, face_number]
            )
        else:
            north_cells = jnp.where(
                at_top, above_layers[:, :, (face_number + 1) % 6], above_layers[:, :, face_number]
            )
            north_speed = jnp.where(
                at_top, above_wind[:, (face_number + 1) % 6], above_wind[:, face_number]
            )
            south_cells = jnp.where(
                at_bottom,
                edge_layers[:, :, (half - 1) % 3],
                below_layers[:, :, face_number],
            )
            south_speed = jnp.where(
                at_bottom,
                edge_speed[:, (half - 1) % 3],
                below_wind[:, face_number],
            )
        south_faces.append(south_cells)
        north_faces.append(north_cells)
        south_speeds.append(south_speed)
        north_speeds.append(north_speed)
    padded = jnp.concatenate(
        [jnp.stack(south_faces, 2), tracer, jnp.stack(north_faces, 2)], -2
    )
    if faces_known is None:
        speeds = jnp.concatenate(
            [
                jnp.stack(south_speeds, 1)[:, :, None, :],
                north_wind,
                jnp.stack(north_speeds, 1)[:, :, None, :],
            ],
            -2,
        )
        faces_known = 0.5 * (speeds[:, :, :-1, :] + speeds[:, :, 1:, :])
    return (padded, faces_known, row_wind, extra)


def regrid(tracer, tile_source, tile_target, intersection, band_count):
    scenarios = tracer.shape[0]
    levels = tracer.shape[1]
    batch_rows = scenarios * levels
    block_cells = intersection.shape[1]
    blocks = tracer.astype(jnp.bfloat16).reshape(batch_rows, -1, block_cells)
    chosen = jnp.take(blocks, tile_source, axis=1)
    partial_value = jnp.einsum(
        "btk,tkc->tbc", chosen, intersection, preferred_element_type=jnp.float32
    )
    target_band = tile_target // TGT_DEV
    target_block = tile_target % TGT_DEV
    band_hot = (target_band[:, None] == jnp.arange(band_count)[None, :]).astype(jnp.int32)
    rank = jnp.sum((jnp.cumsum(band_hot, 0) - band_hot) * band_hot, 1)
    slot = jnp.where(rank < SLOTS, target_band * SLOTS + rank, -1)
    slot_hot = (slot[None, :] == jnp.arange(band_count * SLOTS)[:, None]).astype(jnp.float32)
    slotted = jnp.einsum(
        "st,tbc->sbc", slot_hot, partial_value, precision=lax.Precision.HIGHEST
    )
    slot_block = jnp.sum(slot_hot * target_block[None, :].astype(jnp.float32), 1)
    index_rows = jnp.zeros((band_count, 8, block_cells), jnp.float32)
    index_rows = index_rows.at[:, 0, :SLOTS].set(slot_block.reshape(band_count, SLOTS))
    send = jnp.concatenate(
        [slotted.reshape(band_count, SLOTS * batch_rows, block_cells), index_rows], 1
    )
    got = lax.all_to_all(send, "space", 0, 0, tiled=True)
    values = got[:, : SLOTS * batch_rows].reshape(band_count * SLOTS, batch_rows, block_cells)
    got_block = got[:, SLOTS * batch_rows, :SLOTS].reshape(-1)
    block_hot = (got_block[None, :] == jnp.arange(TGT_DEV)[:, None].astype(jnp.float32)).astype(
        jnp.float32
    )
    summed = jnp.einsum("ks,sbc->bkc", block_hot, values, precision=lax.Precision.HIGHEST)
    return summed.reshape(scenarios, levels, TGT_DEV, block_cells)


def moments_of(regridded):
    scenarios = regridded.shape[0]
    scen_count = lax.axis_size("scen")
    copies = jnp.broadcast_to(regridded, (scen_count,) + regridded.shape[1:])
    everyone = lax.all_to_all(copies, "scen", 0, 0, tiled=True)
    moment_sums = jnp.stack([jnp.sum(everyone, 0), jnp.sum(everyone * everyone, 0)])
    return moment_sums / (scenarios * scen_count)


def local(concentration, emissions, courant, tile_source, tile_target, intersection):
    band_count = lax.axis_size("space")
    position = lax.axis_index("space")
    tracer = concentration.at[:, 0].add(emissions)
    east_wind = courant[0]
    north_wind = courant[1]
    top_cells, low_cells, top_wind, low_wind = first_exchange(
        tracer, north_wind, position, band_count
    )
    row_wind = None
    cx = None
    cy = None
    for step_number in range(2):
        padded, cx = column_halos(
            tracer, east_wind, top_cells, low_cells, top_wind, low_wind, cx
        )
        tracer = parabola_sweep(padded, cx, 4)
        padded, cy, row_wind, extra = row_halos(
            tracer, east_wind, north_wind, position, band_count, row_wind, cy, step_number == 0
        )
        if step_number == 0:
            top_cells, low_cells = next_edge_cells(
                tracer, east_wind, extra[0], extra[1], top_wind, low_wind
            )
        tracer = parabola_sweep(padded, cy, 3)
    regridded = regrid(tracer, tile_source, tile_target, intersection, band_count)
    ensemble_moments = moments_of(regridded)
    return (tracer, regridded, ensemble_moments)


def solution(mesh):
    return jax.shard_map(
        local,
        mesh=mesh,
        in_specs=(
            P("scen", None, None, "space", None),
            P("scen", None, "space", None),
            P(None, None, None, "space", None),
            P("space"),
            P("space"),
            P("space", None, None),
        ),
        out_specs=(
            P("scen", None, None, "space", None),
            P("scen", None, "space", None),
            P(None, None, "space", None),
        ),
        check_vma=False,
    )
```

```python
import jax
import jax.numpy as jnp
from jax import lax
from jax.sharding import PartitionSpec as P

TGT_DEV = 32
SLOTS = 16


def from_behind(block, axis, distance):
    devices = range(lax.axis_size(axis))
    route = [((i - distance) % len(devices), i) for i in devices]
    return lax.ppermute(block, axis, route)


def parabola_sweep(padded, courant_faces, sweep_axis):
    cells_along = padded.shape[sweep_axis] - 6

    def window(values_in, first_cell, length):
        return lax.slice_in_dim(values_in, first_cell, first_cell + length, axis=sweep_axis)

    edge_values = 7.0 / 12.0 * (
        window(padded, 1, cells_along + 3) + window(padded, 2, cells_along + 3)
    ) - 1.0 / 12.0 * (window(padded, 0, cells_along + 3) + window(padded, 3, cells_along + 3))
    left_edge = window(edge_values, 0, cells_along + 2)
    right_edge = window(edge_values, 1, cells_along + 2)
    centre = window(padded, 2, cells_along + 2)
    slopes = right_edge - left_edge
    curvature = 6.0 * centre - 3.0 * (left_edge + right_edge)
    backward = -courant_faces
    upwind_left = courant_faces * (
        window(right_edge, 0, cells_along + 1)
        - 0.5
        * courant_faces
        * (
            window(slopes, 0, cells_along + 1)
            - (1.0 - 2.0 * courant_faces / 3.0) * window(curvature, 0, cells_along + 1)
        )
    )
    upwind_right = courant_faces * (
        window(left_edge, 1, cells_along + 1)
        + 0.5
        * backward
        * (
            window(slopes, 1, cells_along + 1)
            + (1.0 - 2.0 * backward / 3.0) * window(curvature, 1, cells_along + 1)
        )
    )
    fluxes = jnp.where(courant_faces >= 0.0, upwind_left, upwind_right)
    return window(padded, 3, cells_along) - (
        window(fluxes, 1, cells_along) - window(fluxes, 0, cells_along)
    )


def pack_rows(tracer, north_wind, lowest):
    row_count = tracer.shape[3]
    width_cells = tracer.shape[4]
    if lowest:
        layers = tracer[:, :, :, 0:3, :]
    else:
        layers = tracer[:, :, :, row_count - 3 :, :]
    parts = [layers.reshape(-1, width_cells)]
    if north_wind is not None:
        wind_row = north_wind[:, :, 0:1, :] if lowest else north_wind[:, :, row_count - 1 :, :]
        parts.append(wind_row.reshape(-1, width_cells))
    return jnp.concatenate(parts, 0)


def first_exchange(tracer, north_wind, position, band_count):
    scenarios, levels, _, row_count, width_cells = tracer.shape
    top = jnp.concatenate(
        [
            tracer[:, :, 0::2, row_count - 3 :, :].reshape(-1, width_cells),
            north_wind[:, 0::2, row_count - 4 :, :].reshape(-1, width_cells),
        ],
        0,
    )
    low = jnp.concatenate(
        [
            tracer[:, :, 1::2, 0:3, :].reshape(-1, width_cells),
            north_wind[:, 1::2, 0:4, :].reshape(-1, width_cells),
        ],
        0,
    )
    send = jnp.where(position == band_count - 1, top, jnp.where(position == 0, low, 0.0))
    send = jnp.flip(send.T, 0).reshape(band_count, -1)
    got = lax.all_to_all(send, "space", 0, 0, tiled=True)
    count = top.shape[0]
    cells = scenarios * levels * 3 * 3

    def cells_of(block):
        return block[:, :cells].reshape(row_count, scenarios, levels, 3, 3)

    def wind_of(block):
        return block[:, cells:].reshape(row_count, levels, 3, 4)

    top_got = got[band_count - 1].reshape(row_count, count)
    low_got = got[0].reshape(row_count, count)
    return cells_of(top_got), cells_of(low_got), wind_of(top_got), wind_of(low_got)


def next_edge_cells(swept, east_wind, rows_top, rows_low, top_wind, low_wind):
    width_cells = swept.shape[4]
    halo_top = jnp.stack(
        [jnp.moveaxis(swept[:, :, (2 * e + 2) % 6, :, 0:3], 2, 0) for e in range(3)], 3
    )
    halo_low = jnp.stack(
        [jnp.moveaxis(swept[:, :, (2 * o - 1) % 6, :, width_cells - 3 :], 2, 0) for o in range(3)],
        3,
    )
    speed_top = jnp.stack([east_wind[:, (2 * e + 2) % 6, :, 0].T for e in range(3)], 2)
    speed_low = jnp.stack([east_wind[:, (2 * o - 1) % 6, :, width_cells - 1].T for o in range(3)], 2)
    speeds_top = jnp.concatenate([top_wind, speed_top[..., None]], -1)
    speeds_low = jnp.concatenate([speed_low[..., None], low_wind], -1)
    faces_top = 0.5 * (speeds_top[..., :-1] + speeds_top[..., 1:])
    faces_low = 0.5 * (speeds_low[..., :-1] + speeds_low[..., 1:])
    top_cells = parabola_sweep(
        jnp.concatenate([rows_top, halo_top], -1), faces_top[:, None], 4
    )
    low_cells = parabola_sweep(
        jnp.concatenate([halo_low, rows_low], -1), faces_low[:, None], 4
    )
    return top_cells, low_cells


def column_halos(tracer, east_wind, top_cells, low_cells, top_wind, low_wind, faces_known):
    width_cells = tracer.shape[4]
    west_faces, east_faces, west_speeds, east_speeds = [], [], [], []
    for face_number in range(6):
        half = face_number // 2
        if face_number % 2 == 0:
            west_cells = jnp.moveaxis(top_cells[:, :, :, (half - 1) % 3], 0, 2)
            west_speed = top_wind[:, :, (half - 1) % 3, 3].T
            east_cells = tracer[:, :, (face_number + 1) % 6, :, 0:3]
            east_speed = east_wind[:, (face_number + 1) % 6, :, 0]
        else:
            west_cells = tracer[:, :, (face_number - 1) % 6, :, width_cells - 3 :]
            west_speed = east_wind[:, (face_number - 1) % 6, :, width_cells - 1]
            east_cells = jnp.moveaxis(low_cells[:, :, :, (half + 1) % 3], 0, 2)
            east_speed = low_wind[:, :, (half + 1) % 3, 0].T
        west_faces.append(west_cells)
        east_faces.append(east_cells)
        west_speeds.append(west_speed)
        east_speeds.append(east_speed)
    padded = jnp.concatenate(
        [jnp.stack(west_faces, 2), tracer, jnp.stack(east_faces, 2)], -1
    )
    if faces_known is None:
        speeds = jnp.concatenate(
            [
                jnp.stack(west_speeds, 1)[..., None],
                east_wind,
                jnp.stack(east_speeds, 1)[..., None],
            ],
            -1,
        )
        faces_known = 0.5 * (speeds[..., :-1] + speeds[..., 1:])
    return padded, faces_known


def edge_columns(tracer, east_wind, position, band_count, with_wind, scatter_rows):
    scenarios, levels, _, row_count, width_cells = tracer.shape
    to_top = [jnp.moveaxis(tracer[:, :, 0::2, :, 0:3], 3, 0).reshape(row_count, -1)]
    to_low = [jnp.moveaxis(tracer[:, :, 1::2, :, width_cells - 3 :], 3, 0).reshape(row_count, -1)]
    if with_wind:
        to_top.append(jnp.moveaxis(east_wind[:, 0::2, :, 0], 2, 0).reshape(row_count, -1))
        to_low.append(
            jnp.moveaxis(east_wind[:, 1::2, :, width_cells - 1], 2, 0).reshape(row_count, -1)
        )
    to_top = jnp.concatenate(to_top, 1)
    to_low = jnp.concatenate(to_low, 1)
    count = to_top.shape[1]
    send = jnp.zeros((band_count, row_count, count), to_top.dtype)
    send = send.at[band_count - 1].set(to_top).at[0].set(to_low)
    if scatter_rows:
        rows_top = tracer[:, :, 0::2, row_count - 6 :, :].reshape(-1, width_cells)
        rows_low = tracer[:, :, 1::2, 0:6, :].reshape(-1, width_cells)
        chosen = jnp.where(
            position == band_count - 1, rows_top, jnp.where(position == 0, rows_low, 0.0)
        )
        scattered = jnp.flip(chosen.T, 0).reshape(band_count, row_count, rows_top.shape[0])
        send = jnp.concatenate([send, scattered], 2)
    got = lax.all_to_all(send, "space", 0, 0, tiled=True)
    extra = None
    if scatter_rows:

        def rows_of(block):
            return block.reshape(row_count, scenarios, levels, 3, 6)

        extra = (rows_of(got[band_count - 1, :, count:]), rows_of(got[0, :, count:]))
        got = got[:, :, :count]
    flipped = jnp.flip(got.reshape(-1, count), 0).T
    cells = scenarios * levels * 3 * 3
    layers = flipped[:cells].reshape(scenarios, levels, 3, 3, band_count * row_count)
    wind = None
    if with_wind:
        wind = flipped[cells:].reshape(levels, 3, band_count * row_count)
    return layers, wind, extra


def row_halos(
    tracer, east_wind, north_wind, position, band_count, row_wind, faces_known, scatter_rows
):
    first_step = row_wind is None
    shifted = []
    for step_by, lowest in ((-1, True), (1, False)):
        packed = pack_rows(tracer, north_wind if first_step else None, lowest)
        shifted.append(from_behind(packed, "space", step_by))
    edge_layers, edge_speed, extra = edge_columns(
        tracer, east_wind, position, band_count, first_step, scatter_rows
    )
    layer_rows = tracer.shape[0] * tracer.shape[1] * 18
    width_cells = tracer.shape[4]
    if first_step:
        levels = tracer.shape[1]
        row_wind = tuple(
            packed[layer_rows:].reshape(levels, 6, width_cells) for packed in shifted
        ) + (edge_speed,)
    above_wind, below_wind, edge_speed = row_wind
    above_layers, below_layers = (
        packed[:layer_rows].reshape(tracer.shape[0], tracer.shape[1], 6, 3, width_cells)
        for packed in shifted
    )
    at_top = position == band_count - 1
    at_bottom = position == 0
    south_faces, north_faces, south_speeds, north_speeds = [], [], [], []
    for face_number in range(6):
        half = face_number // 2
        if face_number % 2 == 0:
            north_cells = jnp.where(
                at_top,
                edge_layers[:, :, (half + 1) % 3],
                above_layers[:, :, face_number],
            )
            north_speed = jnp.where(
                at_top,
                edge_speed[:, (half + 1) % 3],
                above_wind[:, face_number],
            )
            south_cells = jnp.where(
                at_bottom,
                below_layers[:, :, (face_number - 1) % 6],
                below_layers[:, :, face_number],
            )
            south_speed = jnp.where(
                at_bottom, below_wind[:, (face_number - 1) % 6], below_wind[:, face_number]
            )
        else:
            north_cells = jnp.where(
                at_top, above_layers[:, :, (face_number + 1) % 6], above_layers[:, :, face_number]
            )
            north_speed = jnp.where(
                at_top, above_wind[:, (face_number + 1) % 6], above_wind[:, face_number]
            )
            south_cells = jnp.where(
                at_bottom,
                edge_layers[:, :, (half - 1) % 3],
                below_layers[:, :, face_number],
            )
            south_speed = jnp.where(
                at_bottom,
                edge_speed[:, (half - 1) % 3],
                below_wind[:, face_number],
            )
        south_faces.append(south_cells)
        north_faces.append(north_cells)
        south_speeds.append(south_speed)
        north_speeds.append(north_speed)
    padded = jnp.concatenate(
        [jnp.stack(south_faces, 2), tracer, jnp.stack(north_faces, 2)], -2
    )
    if faces_known is None:
        speeds = jnp.concatenate(
            [
                jnp.stack(south_speeds, 1)[:, :, None, :],
                north_wind,
                jnp.stack(north_speeds, 1)[:, :, None, :],
            ],
            -2,
        )
        faces_known = 0.5 * (speeds[:, :, :-1, :] + speeds[:, :, 1:, :])
    return (padded, faces_known, row_wind, extra)


def regrid(tracer, tile_source, tile_target, intersection, band_count):
    scenarios = tracer.shape[0]
    levels = tracer.shape[1]
    batch_rows = scenarios * levels
    block_cells = intersection.shape[1]
    blocks = tracer.astype(jnp.bfloat16).reshape(batch_rows, -1, block_cells)
    chosen = jnp.take(blocks, tile_source, axis=1)
    partial_value = jnp.einsum(
        "btk,tkc->tbc", chosen, intersection, preferred_element_type=jnp.float32
    )
    target_band = tile_target // TGT_DEV
    target_block = tile_target % TGT_DEV
    band_hot = (target_band[:, None] == jnp.arange(band_count)[None, :]).astype(jnp.int32)
    rank = jnp.sum((jnp.cumsum(band_hot, 0) - band_hot) * band_hot, 1)
    slot = jnp.where(rank < SLOTS, target_band * SLOTS + rank, -1)
    slot_hot = (slot[None, :] == jnp.arange(band_count * SLOTS)[:, None]).astype(jnp.float32)
    slotted = jnp.einsum(
        "st,tbc->sbc", slot_hot, partial_value, precision=lax.Precision.HIGHEST
    )
    slot_block = jnp.sum(slot_hot * target_block[None, :].astype(jnp.float32), 1)
    index_rows = jnp.zeros((band_count, 8, block_cells), jnp.float32)
    index_rows = index_rows.at[:, 0, :SLOTS].set(slot_block.reshape(band_count, SLOTS))
    send = jnp.concatenate(
        [slotted.reshape(band_count, SLOTS * batch_rows, block_cells), index_rows], 1
    )
    got = lax.all_to_all(send, "space", 0, 0, tiled=True)
    values = got[:, : SLOTS * batch_rows].reshape(band_count * SLOTS, batch_rows, block_cells)
    got_block = got[:, SLOTS * batch_rows, :SLOTS].reshape(-1)
    block_hot = (got_block[None, :] == jnp.arange(TGT_DEV)[:, None].astype(jnp.float32)).astype(
        jnp.float32
    )
    summed = jnp.einsum("ks,sbc->bkc", block_hot, values, precision=lax.Precision.HIGHEST)
    return summed.reshape(scenarios, levels, TGT_DEV, block_cells)


def moments_of(regridded):
    scenarios = regridded.shape[0]
    scen_count = lax.axis_size("scen")
    copies = jnp.broadcast_to(regridded, (scen_count,) + regridded.shape[1:])
    everyone = lax.all_to_all(copies, "scen", 0, 0, tiled=True)
    moment_sums = jnp.stack([jnp.sum(everyone, 0), jnp.sum(everyone * everyone, 0)])
    return moment_sums / (scenarios * scen_count)


def local(concentration, emissions, courant, tile_source, tile_target, intersection):
    band_count = lax.axis_size("space")
    position = lax.axis_index("space")
    tracer = concentration.at[:, 0].add(emissions)
    east_wind = courant[0]
    north_wind = courant[1]
    top_cells, low_cells, top_wind, low_wind = first_exchange(
        tracer, north_wind, position, band_count
    )
    row_wind = None
    cx = None
    cy = None
    for step_number in range(2):
        padded, cx = column_halos(
            tracer, east_wind, top_cells, low_cells, top_wind, low_wind, cx
        )
        tracer = parabola_sweep(padded, cx, 4)
        padded, cy, row_wind, extra = row_halos(
            tracer, east_wind, north_wind, position, band_count, row_wind, cy, step_number == 0
        )
        if step_number == 0:
            top_cells, low_cells = next_edge_cells(
                tracer, east_wind, extra[0], extra[1], top_wind, low_wind
            )
        tracer = parabola_sweep(padded, cy, 3)
    regridded = regrid(tracer, tile_source, tile_target, intersection, band_count)
    ensemble_moments = moments_of(regridded)
    return (tracer, regridded, ensemble_moments)


def solution(mesh):
    return jax.shard_map(
        local,
        mesh=mesh,
        in_specs=(
            P("scen", None, None, "space", None),
            P("scen", None, "space", None),
            P(None, None, None, "space", None),
            P("space"),
            P("space"),
            P("space", None, None),
        ),
        out_specs=(
            P("scen", None, None, "space", None),
            P("scen", None, "space", None),
            P(None, None, "space", None),
        ),
        check_vma=False,
    )
```

```python
import jax
import jax.numpy as jnp
from jax import lax
from jax.sharding import PartitionSpec as P

TGT_DEV = 32
SLOTS = 16


def from_behind(block, axis, distance):
    devices = range(lax.axis_size(axis))
    route = [((i - distance) % len(devices), i) for i in devices]
    return lax.ppermute(block, axis, route)


def parabola_sweep(padded, courant_faces, sweep_axis):
    cells_along = padded.shape[sweep_axis] - 6

    def window(values_in, first_cell, length):
        return lax.slice_in_dim(values_in, first_cell, first_cell + length, axis=sweep_axis)

    edge_values = 7.0 / 12.0 * (
        window(padded, 1, cells_along + 3) + window(padded, 2, cells_along + 3)
    ) - 1.0 / 12.0 * (window(padded, 0, cells_along + 3) + window(padded, 3, cells_along + 3))
    left_edge = window(edge_values, 0, cells_along + 2)
    right_edge = window(edge_values, 1, cells_along + 2)
    centre = window(padded, 2, cells_along + 2)
    slopes = right_edge - left_edge
    curvature = 6.0 * centre - 3.0 * (left_edge + right_edge)
    backward = -courant_faces
    upwind_left = courant_faces * (
        window(right_edge, 0, cells_along + 1)
        - 0.5
        * courant_faces
        * (
            window(slopes, 0, cells_along + 1)
            - (1.0 - 2.0 * courant_faces / 3.0) * window(curvature, 0, cells_along + 1)
        )
    )
    upwind_right = courant_faces * (
        window(left_edge, 1, cells_along + 1)
        + 0.5
        * backward
        * (
            window(slopes, 1, cells_along + 1)
            + (1.0 - 2.0 * backward / 3.0) * window(curvature, 1, cells_along + 1)
        )
    )
    fluxes = jnp.where(courant_faces >= 0.0, upwind_left, upwind_right)
    return window(padded, 3, cells_along) - (
        window(fluxes, 1, cells_along) - window(fluxes, 0, cells_along)
    )


def pack_rows(tracer, north_wind, lowest):
    row_count = tracer.shape[3]
    width_cells = tracer.shape[4]
    if lowest:
        layers = tracer[:, :, :, 0:3, :]
    else:
        layers = tracer[:, :, :, row_count - 3 :, :]
    parts = [layers.reshape(-1, width_cells)]
    if north_wind is not None:
        wind_row = north_wind[:, :, 0:1, :] if lowest else north_wind[:, :, row_count - 1 :, :]
        parts.append(wind_row.reshape(-1, width_cells))
    return jnp.concatenate(parts, 0)


def edge_rows(tracer, north_wind, position, band_count, with_wind):
    row_count = tracer.shape[3]
    width_cells = tracer.shape[4]
    top = [tracer[:, :, 0::2, row_count - 3 :, :].reshape(-1, width_cells)]
    low = [tracer[:, :, 1::2, 0:3, :].reshape(-1, width_cells)]
    if with_wind:
        top.append(north_wind[:, 0::2, row_count - 1, :].reshape(-1, width_cells))
        low.append(north_wind[:, 1::2, 0, :].reshape(-1, width_cells))
    top = jnp.concatenate(top, 0)
    low = jnp.concatenate(low, 0)
    send = jnp.where(position == band_count - 1, top, jnp.where(position == 0, low, 0.0))
    send = jnp.flip(send.T, 0).reshape(band_count, -1)
    got = lax.all_to_all(send, "space", 0, 0, tiled=True)
    count = top.shape[0]
    return got[band_count - 1].reshape(-1, count), got[0].reshape(-1, count)


def column_halos(tracer, east_wind, north_wind, position, band_count, edge_wind, faces_known):
    scenarios, levels, _, row_count, width_cells = tracer.shape
    top, low = edge_rows(tracer, north_wind, position, band_count, edge_wind is None)
    cells = scenarios * levels * 3 * 3
    top_layers = top[:, :cells].reshape(row_count, scenarios, levels, 3, 3)
    low_layers = low[:, :cells].reshape(row_count, scenarios, levels, 3, 3)
    if edge_wind is None:
        edge_wind = (
            top[:, cells:].reshape(row_count, levels, 3),
            low[:, cells:].reshape(row_count, levels, 3),
        )
    top_wind, low_wind = edge_wind
    west_faces, east_faces, west_speeds, east_speeds = [], [], [], []
    for face_number in range(6):
        half = face_number // 2
        if face_number % 2 == 0:
            west_cells = jnp.moveaxis(top_layers[:, :, :, (half - 1) % 3], 0, 2)
            west_speed = top_wind[:, :, (half - 1) % 3].T
            east_cells = tracer[:, :, (face_number + 1) % 6, :, 0:3]
            east_speed = east_wind[:, (face_number + 1) % 6, :, 0]
        else:
            west_cells = tracer[:, :, (face_number - 1) % 6, :, width_cells - 3 :]
            west_speed = east_wind[:, (face_number - 1) % 6, :, width_cells - 1]
            east_cells = jnp.moveaxis(low_layers[:, :, :, (half + 1) % 3], 0, 2)
            east_speed = low_wind[:, :, (half + 1) % 3].T
        west_faces.append(west_cells)
        east_faces.append(east_cells)
        west_speeds.append(west_speed)
        east_speeds.append(east_speed)
    padded = jnp.concatenate(
        [jnp.stack(west_faces, 2), tracer, jnp.stack(east_faces, 2)], -1
    )
    if faces_known is None:
        speeds = jnp.concatenate(
            [
                jnp.stack(west_speeds, 1)[..., None],
                east_wind,
                jnp.stack(east_speeds, 1)[..., None],
            ],
            -1,
        )
        faces_known = 0.5 * (speeds[..., :-1] + speeds[..., 1:])
    return (padded, faces_known, edge_wind)


def edge_columns(tracer, east_wind, position, band_count, with_wind):
    scenarios, levels, _, row_count, width_cells = tracer.shape
    to_top = [jnp.moveaxis(tracer[:, :, 0::2, :, 0:3], 3, 0).reshape(row_count, -1)]
    to_low = [jnp.moveaxis(tracer[:, :, 1::2, :, width_cells - 3 :], 3, 0).reshape(row_count, -1)]
    if with_wind:
        to_top.append(jnp.moveaxis(east_wind[:, 0::2, :, 0], 2, 0).reshape(row_count, -1))
        to_low.append(
            jnp.moveaxis(east_wind[:, 1::2, :, width_cells - 1], 2, 0).reshape(row_count, -1)
        )
    to_top = jnp.concatenate(to_top, 1)
    to_low = jnp.concatenate(to_low, 1)
    count = to_top.shape[1]
    destination = lax.broadcasted_iota(jnp.int32, (band_count, row_count, count), 0)
    send = jnp.where(
        destination == band_count - 1, to_top[None], jnp.where(destination == 0, to_low[None], 0.0)
    ).astype(to_top.dtype)
    got = lax.all_to_all(send, "space", 0, 0, tiled=True)
    flipped = jnp.flip(got.reshape(-1, count), 0).T
    cells = scenarios * levels * 3 * 3
    layers = flipped[:cells].reshape(scenarios, levels, 3, 3, band_count * row_count)
    wind = None
    if with_wind:
        wind = flipped[cells:].reshape(levels, 3, band_count * row_count)
    return layers, wind


def row_halos(tracer, east_wind, north_wind, position, band_count, row_wind, faces_known):
    first_step = row_wind is None
    shifted = []
    for step_by, lowest in ((-1, True), (1, False)):
        packed = pack_rows(tracer, north_wind if first_step else None, lowest)
        shifted.append(from_behind(packed, "space", step_by))
    edge_layers, edge_speed = edge_columns(tracer, east_wind, position, band_count, first_step)
    layer_rows = tracer.shape[0] * tracer.shape[1] * 18
    width_cells = tracer.shape[4]
    if first_step:
        levels = tracer.shape[1]
        row_wind = tuple(
            packed[layer_rows:].reshape(levels, 6, width_cells) for packed in shifted
        ) + (edge_speed,)
    above_wind, below_wind, edge_speed = row_wind
    above_layers, below_layers = (
        packed[:layer_rows].reshape(tracer.shape[0], tracer.shape[1], 6, 3, width_cells)
        for packed in shifted
    )
    at_top = position == band_count - 1
    at_bottom = position == 0
    south_faces, north_faces, south_speeds, north_speeds = [], [], [], []
    for face_number in range(6):
        half = face_number // 2
        if face_number % 2 == 0:
            north_cells = jnp.where(
                at_top,
                edge_layers[:, :, (half + 1) % 3],
                above_layers[:, :, face_number],
            )
            north_speed = jnp.where(
                at_top,
                edge_speed[:, (half + 1) % 3],
                above_wind[:, face_number],
            )
            south_cells = jnp.where(
                at_bottom,
                below_layers[:, :, (face_number - 1) % 6],
                below_layers[:, :, face_number],
            )
            south_speed = jnp.where(
                at_bottom, below_wind[:, (face_number - 1) % 6], below_wind[:, face_number]
            )
        else:
            north_cells = jnp.where(
                at_top, above_layers[:, :, (face_number + 1) % 6], above_layers[:, :, face_number]
            )
            north_speed = jnp.where(
                at_top, above_wind[:, (face_number + 1) % 6], above_wind[:, face_number]
            )
            south_cells = jnp.where(
                at_bottom,
                edge_layers[:, :, (half - 1) % 3],
                below_layers[:, :, face_number],
            )
            south_speed = jnp.where(
                at_bottom,
                edge_speed[:, (half - 1) % 3],
                below_wind[:, face_number],
            )
        south_faces.append(south_cells)
        north_faces.append(north_cells)
        south_speeds.append(south_speed)
        north_speeds.append(north_speed)
    padded = jnp.concatenate(
        [jnp.stack(south_faces, 2), tracer, jnp.stack(north_faces, 2)], -2
    )
    if faces_known is None:
        speeds = jnp.concatenate(
            [
                jnp.stack(south_speeds, 1)[:, :, None, :],
                north_wind,
                jnp.stack(north_speeds, 1)[:, :, None, :],
            ],
            -2,
        )
        faces_known = 0.5 * (speeds[:, :, :-1, :] + speeds[:, :, 1:, :])
    return (padded, faces_known, row_wind)


def regrid(tracer, tile_source, tile_target, intersection, band_count):
    scenarios = tracer.shape[0]
    levels = tracer.shape[1]
    batch_rows = scenarios * levels
    block_cells = intersection.shape[1]
    blocks = tracer.astype(jnp.bfloat16).reshape(batch_rows, -1, block_cells)
    chosen = jnp.take(blocks, tile_source, axis=1)
    partial_value = jnp.einsum(
        "btk,tkc->tbc", chosen, intersection, preferred_element_type=jnp.float32
    )
    target_band = tile_target // TGT_DEV
    target_block = tile_target % TGT_DEV
    band_hot = (target_band[:, None] == jnp.arange(band_count)[None, :]).astype(jnp.int32)
    rank = jnp.sum((jnp.cumsum(band_hot, 0) - band_hot) * band_hot, 1)
    slot = jnp.where(rank < SLOTS, target_band * SLOTS + rank, -1)
    slot_hot = (slot[None, :] == jnp.arange(band_count * SLOTS)[:, None]).astype(jnp.float32)
    slotted = jnp.einsum(
        "st,tbc->sbc", slot_hot, partial_value, precision=lax.Precision.HIGHEST
    )
    slot_block = jnp.sum(slot_hot * target_block[None, :].astype(jnp.float32), 1)
    index_rows = jnp.zeros((band_count, 8, block_cells), jnp.float32)
    index_rows = index_rows.at[:, 0, :SLOTS].set(slot_block.reshape(band_count, SLOTS))
    send = jnp.concatenate(
        [slotted.reshape(band_count, SLOTS * batch_rows, block_cells), index_rows], 1
    )
    got = lax.all_to_all(send, "space", 0, 0, tiled=True)
    values = got[:, : SLOTS * batch_rows].reshape(band_count * SLOTS, batch_rows, block_cells)
    got_block = got[:, SLOTS * batch_rows, :SLOTS].reshape(-1)
    block_hot = (got_block[None, :] == jnp.arange(TGT_DEV)[:, None].astype(jnp.float32)).astype(
        jnp.float32
    )
    summed = jnp.einsum("ks,sbc->bkc", block_hot, values, precision=lax.Precision.HIGHEST)
    return summed.reshape(scenarios, levels, TGT_DEV, block_cells)


def moments_of(regridded):
    scenarios = regridded.shape[0]
    scen_count = lax.axis_size("scen")
    copies = jnp.broadcast_to(regridded, (scen_count,) + regridded.shape[1:])
    everyone = lax.all_to_all(copies, "scen", 0, 0, tiled=True)
    moment_sums = jnp.stack([jnp.sum(everyone, 0), jnp.sum(everyone * everyone, 0)])
    return moment_sums / (scenarios * scen_count)


def local(concentration, emissions, courant, tile_source, tile_target, intersection):
    band_count = lax.axis_size("space")
    position = lax.axis_index("space")
    tracer = concentration.at[:, 0].add(emissions)
    east_wind = courant[0]
    north_wind = courant[1]
    edge_wind = None
    row_wind = None
    cx = None
    cy = None
    for step_number in range(2):
        padded, cx, edge_wind = column_halos(
            tracer, east_wind, north_wind, position, band_count, edge_wind, cx
        )
        tracer = parabola_sweep(padded, cx, 4)
        padded, cy, row_wind = row_halos(
            tracer, east_wind, north_wind, position, band_count, row_wind, cy
        )
        tracer = parabola_sweep(padded, cy, 3)
    regridded = regrid(tracer, tile_source, tile_target, intersection, band_count)
    ensemble_moments = moments_of(regridded)
    return (tracer, regridded, ensemble_moments)


def solution(mesh):
    return jax.shard_map(
        local,
        mesh=mesh,
        in_specs=(
            P("scen", None, None, "space", None),
            P("scen", None, "space", None),
            P(None, None, None, "space", None),
            P("space"),
            P("space"),
            P("space", None, None),
        ),
        out_specs=(
            P("scen", None, None, "space", None),
            P("scen", None, "space", None),
            P(None, None, "space", None),
        ),
        check_vma=False,
    )
```

```python
import jax
import jax.numpy as jnp
from jax import lax
from jax.sharding import PartitionSpec as P

TGT_DEV = 32
SLOTS = 16


def from_behind(block, axis, distance):
    devices = range(lax.axis_size(axis))
    route = [((i - distance) % len(devices), i) for i in devices]
    return lax.ppermute(block, axis, route)


def parabola_sweep(padded, courant_faces, sweep_axis):
    cells_along = padded.shape[sweep_axis] - 6

    def window(values_in, first_cell, length):
        return lax.slice_in_dim(values_in, first_cell, first_cell + length, axis=sweep_axis)

    edge_values = 7.0 / 12.0 * (
        window(padded, 1, cells_along + 3) + window(padded, 2, cells_along + 3)
    ) - 1.0 / 12.0 * (window(padded, 0, cells_along + 3) + window(padded, 3, cells_along + 3))
    left_edge = window(edge_values, 0, cells_along + 2)
    right_edge = window(edge_values, 1, cells_along + 2)
    centre = window(padded, 2, cells_along + 2)
    slopes = right_edge - left_edge
    curvature = 6.0 * centre - 3.0 * (left_edge + right_edge)
    backward = -courant_faces
    upwind_left = courant_faces * (
        window(right_edge, 0, cells_along + 1)
        - 0.5
        * courant_faces
        * (
            window(slopes, 0, cells_along + 1)
            - (1.0 - 2.0 * courant_faces / 3.0) * window(curvature, 0, cells_along + 1)
        )
    )
    upwind_right = courant_faces * (
        window(left_edge, 1, cells_along + 1)
        + 0.5
        * backward
        * (
            window(slopes, 1, cells_along + 1)
            + (1.0 - 2.0 * backward / 3.0) * window(curvature, 1, cells_along + 1)
        )
    )
    fluxes = jnp.where(courant_faces >= 0.0, upwind_left, upwind_right)
    return window(padded, 3, cells_along) - (
        window(fluxes, 1, cells_along) - window(fluxes, 0, cells_along)
    )


def pack_rows(tracer, north_wind, lowest):
    row_count = tracer.shape[3]
    width_cells = tracer.shape[4]
    if lowest:
        layers = tracer[:, :, :, 0:3, :]
    else:
        layers = tracer[:, :, :, row_count - 3 :, :]
    parts = [layers.reshape(-1, width_cells)]
    if north_wind is not None:
        wind_row = north_wind[:, :, 0:1, :] if lowest else north_wind[:, :, row_count - 1 :, :]
        parts.append(wind_row.reshape(-1, width_cells))
    return jnp.concatenate(parts, 0)


def edge_rows(tracer, north_wind, position, band_count, with_wind):
    row_count = tracer.shape[3]
    width_cells = tracer.shape[4]
    top = [tracer[:, :, 0::2, row_count - 3 :, :].reshape(-1, width_cells)]
    low = [tracer[:, :, 1::2, 0:3, :].reshape(-1, width_cells)]
    if with_wind:
        top.append(north_wind[:, 0::2, row_count - 1, :].reshape(-1, width_cells))
        low.append(north_wind[:, 1::2, 0, :].reshape(-1, width_cells))
    top = jnp.concatenate(top, 0)
    low = jnp.concatenate(low, 0)
    send = jnp.where(position == band_count - 1, top, jnp.where(position == 0, low, 0.0))
    count = top.shape[0]
    send = jnp.flip(send.T.reshape(band_count, -1, count), 0).reshape(band_count, -1)
    got = lax.all_to_all(send, "space", 0, 0, tiled=True)
    return (
        jnp.flip(got[band_count - 1].reshape(-1, count), 0),
        jnp.flip(got[0].reshape(-1, count), 0),
    )


def column_halos(tracer, east_wind, north_wind, position, band_count, edge_wind, faces_known):
    scenarios, levels, _, row_count, width_cells = tracer.shape
    top, low = edge_rows(tracer, north_wind, position, band_count, edge_wind is None)
    cells = scenarios * levels * 3 * 3
    top_layers = top[:, :cells].reshape(row_count, scenarios, levels, 3, 3)
    low_layers = low[:, :cells].reshape(row_count, scenarios, levels, 3, 3)
    if edge_wind is None:
        edge_wind = (
            top[:, cells:].reshape(row_count, levels, 3),
            low[:, cells:].reshape(row_count, levels, 3),
        )
    top_wind, low_wind = edge_wind
    west_faces, east_faces, west_speeds, east_speeds = [], [], [], []
    for face_number in range(6):
        half = face_number // 2
        if face_number % 2 == 0:
            west_cells = jnp.moveaxis(top_layers[:, :, :, (half - 1) % 3], 0, 2)
            west_speed = top_wind[:, :, (half - 1) % 3].T
            east_cells = tracer[:, :, (face_number + 1) % 6, :, 0:3]
            east_speed = east_wind[:, (face_number + 1) % 6, :, 0]
        else:
            west_cells = tracer[:, :, (face_number - 1) % 6, :, width_cells - 3 :]
            west_speed = east_wind[:, (face_number - 1) % 6, :, width_cells - 1]
            east_cells = jnp.moveaxis(low_layers[:, :, :, (half + 1) % 3], 0, 2)
            east_speed = low_wind[:, :, (half + 1) % 3].T
        west_faces.append(west_cells)
        east_faces.append(east_cells)
        west_speeds.append(west_speed)
        east_speeds.append(east_speed)
    padded = jnp.concatenate(
        [jnp.stack(west_faces, 2), tracer, jnp.stack(east_faces, 2)], -1
    )
    if faces_known is None:
        speeds = jnp.concatenate(
            [
                jnp.stack(west_speeds, 1)[..., None],
                east_wind,
                jnp.stack(east_speeds, 1)[..., None],
            ],
            -1,
        )
        faces_known = 0.5 * (speeds[..., :-1] + speeds[..., 1:])
    return (padded, faces_known, edge_wind)


def edge_columns(tracer, east_wind, position, band_count, with_wind):
    scenarios, levels, _, row_count, width_cells = tracer.shape
    to_top = [jnp.moveaxis(tracer[:, :, 0::2, :, 0:3], 3, 0).reshape(row_count, -1)]
    to_low = [jnp.moveaxis(tracer[:, :, 1::2, :, width_cells - 3 :], 3, 0).reshape(row_count, -1)]
    if with_wind:
        to_top.append(jnp.moveaxis(east_wind[:, 0::2, :, 0], 2, 0).reshape(row_count, -1))
        to_low.append(
            jnp.moveaxis(east_wind[:, 1::2, :, width_cells - 1], 2, 0).reshape(row_count, -1)
        )
    to_top = jnp.flip(jnp.concatenate(to_top, 1), 0)
    to_low = jnp.flip(jnp.concatenate(to_low, 1), 0)
    count = to_top.shape[1]
    destination = lax.broadcasted_iota(jnp.int32, (band_count, row_count, count), 0)
    send = jnp.where(
        destination == band_count - 1, to_top[None], jnp.where(destination == 0, to_low[None], 0.0)
    ).astype(to_top.dtype)
    got = lax.all_to_all(send, "space", 0, 0, tiled=True)
    flipped = jnp.flip(got, 0).reshape(-1, count).T
    cells = scenarios * levels * 3 * 3
    layers = flipped[:cells].reshape(scenarios, levels, 3, 3, band_count * row_count)
    wind = None
    if with_wind:
        wind = flipped[cells:].reshape(levels, 3, band_count * row_count)
    return layers, wind


def row_halos(tracer, east_wind, north_wind, position, band_count, row_wind, faces_known):
    first_step = row_wind is None
    shifted = []
    for step_by, lowest in ((-1, True), (1, False)):
        packed = pack_rows(tracer, north_wind if first_step else None, lowest)
        shifted.append(from_behind(packed, "space", step_by))
    edge_layers, edge_speed = edge_columns(tracer, east_wind, position, band_count, first_step)
    layer_rows = tracer.shape[0] * tracer.shape[1] * 18
    width_cells = tracer.shape[4]
    if first_step:
        levels = tracer.shape[1]
        row_wind = tuple(
            packed[layer_rows:].reshape(levels, 6, width_cells) for packed in shifted
        ) + (edge_speed,)
    above_wind, below_wind, edge_speed = row_wind
    above_layers, below_layers = (
        packed[:layer_rows].reshape(tracer.shape[0], tracer.shape[1], 6, 3, width_cells)
        for packed in shifted
    )
    at_top = position == band_count - 1
    at_bottom = position == 0
    south_faces, north_faces, south_speeds, north_speeds = [], [], [], []
    for face_number in range(6):
        half = face_number // 2
        if face_number % 2 == 0:
            north_cells = jnp.where(
                at_top,
                edge_layers[:, :, (half + 1) % 3],
                above_layers[:, :, face_number],
            )
            north_speed = jnp.where(
                at_top,
                edge_speed[:, (half + 1) % 3],
                above_wind[:, face_number],
            )
            south_cells = jnp.where(
                at_bottom,
                below_layers[:, :, (face_number - 1) % 6],
                below_layers[:, :, face_number],
            )
            south_speed = jnp.where(
                at_bottom, below_wind[:, (face_number - 1) % 6], below_wind[:, face_number]
            )
        else:
            north_cells = jnp.where(
                at_top, above_layers[:, :, (face_number + 1) % 6], above_layers[:, :, face_number]
            )
            north_speed = jnp.where(
                at_top, above_wind[:, (face_number + 1) % 6], above_wind[:, face_number]
            )
            south_cells = jnp.where(
                at_bottom,
                edge_layers[:, :, (half - 1) % 3],
                below_layers[:, :, face_number],
            )
            south_speed = jnp.where(
                at_bottom,
                edge_speed[:, (half - 1) % 3],
                below_wind[:, face_number],
            )
        south_faces.append(south_cells)
        north_faces.append(north_cells)
        south_speeds.append(south_speed)
        north_speeds.append(north_speed)
    padded = jnp.concatenate(
        [jnp.stack(south_faces, 2), tracer, jnp.stack(north_faces, 2)], -2
    )
    if faces_known is None:
        speeds = jnp.concatenate(
            [
                jnp.stack(south_speeds, 1)[:, :, None, :],
                north_wind,
                jnp.stack(north_speeds, 1)[:, :, None, :],
            ],
            -2,
        )
        faces_known = 0.5 * (speeds[:, :, :-1, :] + speeds[:, :, 1:, :])
    return (padded, faces_known, row_wind)


def regrid(tracer, tile_source, tile_target, intersection, band_count):
    scenarios = tracer.shape[0]
    levels = tracer.shape[1]
    batch_rows = scenarios * levels
    block_cells = intersection.shape[1]
    blocks = tracer.astype(jnp.bfloat16).reshape(batch_rows, -1, block_cells)
    chosen = jnp.take(blocks, tile_source, axis=1)
    partial_value = jnp.einsum(
        "btk,tkc->tbc", chosen, intersection, preferred_element_type=jnp.float32
    )
    target_band = tile_target // TGT_DEV
    target_block = tile_target % TGT_DEV
    band_hot = (target_band[:, None] == jnp.arange(band_count)[None, :]).astype(jnp.int32)
    rank = jnp.sum((jnp.cumsum(band_hot, 0) - band_hot) * band_hot, 1)
    slot = jnp.where(rank < SLOTS, target_band * SLOTS + rank, -1)
    slot_hot = (slot[None, :] == jnp.arange(band_count * SLOTS)[:, None]).astype(jnp.float32)
    slotted = jnp.einsum(
        "st,tbc->sbc", slot_hot, partial_value, precision=lax.Precision.HIGHEST
    )
    slot_block = jnp.sum(slot_hot * target_block[None, :].astype(jnp.float32), 1)
    index_rows = jnp.zeros((band_count, 8, block_cells), jnp.float32)
    index_rows = index_rows.at[:, 0, :SLOTS].set(slot_block.reshape(band_count, SLOTS))
    send = jnp.concatenate(
        [slotted.reshape(band_count, SLOTS * batch_rows, block_cells), index_rows], 1
    )
    got = lax.all_to_all(send, "space", 0, 0, tiled=True)
    values = got[:, : SLOTS * batch_rows].reshape(band_count * SLOTS, batch_rows, block_cells)
    got_block = got[:, SLOTS * batch_rows, :SLOTS].reshape(-1)
    block_hot = (got_block[None, :] == jnp.arange(TGT_DEV)[:, None].astype(jnp.float32)).astype(
        jnp.float32
    )
    summed = jnp.einsum("ks,sbc->bkc", block_hot, values, precision=lax.Precision.HIGHEST)
    return summed.reshape(scenarios, levels, TGT_DEV, block_cells)


def moments_of(regridded):
    scenarios = regridded.shape[0]
    scen_count = lax.axis_size("scen")
    copies = jnp.broadcast_to(regridded, (scen_count,) + regridded.shape[1:])
    everyone = lax.all_to_all(copies, "scen", 0, 0, tiled=True)
    moment_sums = jnp.stack([jnp.sum(everyone, 0), jnp.sum(everyone * everyone, 0)])
    return moment_sums / (scenarios * scen_count)


def local(concentration, emissions, courant, tile_source, tile_target, intersection):
    band_count = lax.axis_size("space")
    position = lax.axis_index("space")
    tracer = concentration.at[:, 0].add(emissions)
    east_wind = courant[0]
    north_wind = courant[1]
    edge_wind = None
    row_wind = None
    cx = None
    cy = None
    for step_number in range(2):
        padded, cx, edge_wind = column_halos(
            tracer, east_wind, north_wind, position, band_count, edge_wind, cx
        )
        tracer = parabola_sweep(padded, cx, 4)
        padded, cy, row_wind = row_halos(
            tracer, east_wind, north_wind, position, band_count, row_wind, cy
        )
        tracer = parabola_sweep(padded, cy, 3)
    regridded = regrid(tracer, tile_source, tile_target, intersection, band_count)
    ensemble_moments = moments_of(regridded)
    return (tracer, regridded, ensemble_moments)


def solution(mesh):
    return jax.shard_map(
        local,
        mesh=mesh,
        in_specs=(
            P("scen", None, None, "space", None),
            P("scen", None, "space", None),
            P(None, None, None, "space", None),
            P("space"),
            P("space"),
            P("space", None, None),
        ),
        out_specs=(
            P("scen", None, None, "space", None),
            P("scen", None, "space", None),
            P(None, None, "space", None),
        ),
        check_vma=False,
    )
```

```python
import jax
import jax.numpy as jnp
from jax import lax
from jax.sharding import PartitionSpec as P

TGT_DEV = 32
SLOTS = 16


def from_behind(block, axis, distance):
    devices = range(lax.axis_size(axis))
    route = [((i - distance) % len(devices), i) for i in devices]
    return lax.ppermute(block, axis, route)


def parabola_sweep(padded, courant_faces, sweep_axis):
    cells_along = padded.shape[sweep_axis] - 6

    def window(values_in, first_cell, length):
        return lax.slice_in_dim(values_in, first_cell, first_cell + length, axis=sweep_axis)

    edge_values = 7.0 / 12.0 * (
        window(padded, 1, cells_along + 3) + window(padded, 2, cells_along + 3)
    ) - 1.0 / 12.0 * (window(padded, 0, cells_along + 3) + window(padded, 3, cells_along + 3))
    left_edge = window(edge_values, 0, cells_along + 2)
    right_edge = window(edge_values, 1, cells_along + 2)
    centre = window(padded, 2, cells_along + 2)
    slopes = right_edge - left_edge
    curvature = 6.0 * centre - 3.0 * (left_edge + right_edge)
    backward = -courant_faces
    upwind_left = courant_faces * (
        window(right_edge, 0, cells_along + 1)
        - 0.5
        * courant_faces
        * (
            window(slopes, 0, cells_along + 1)
            - (1.0 - 2.0 * courant_faces / 3.0) * window(curvature, 0, cells_along + 1)
        )
    )
    upwind_right = courant_faces * (
        window(left_edge, 1, cells_along + 1)
        + 0.5
        * backward
        * (
            window(slopes, 1, cells_along + 1)
            + (1.0 - 2.0 * backward / 3.0) * window(curvature, 1, cells_along + 1)
        )
    )
    fluxes = jnp.where(courant_faces >= 0.0, upwind_left, upwind_right)
    return window(padded, 3, cells_along) - (
        window(fluxes, 1, cells_along) - window(fluxes, 0, cells_along)
    )


def pack_rows(tracer, north_wind, lowest):
    row_count = tracer.shape[3]
    width_cells = tracer.shape[4]
    if lowest:
        layers = tracer[:, :, :, 0:3, :]
    else:
        layers = tracer[:, :, :, row_count - 3 :, :]
    parts = [layers.reshape(-1, width_cells)]
    if north_wind is not None:
        wind_row = north_wind[:, :, 0:1, :] if lowest else north_wind[:, :, row_count - 1 :, :]
        parts.append(wind_row.reshape(-1, width_cells))
    return jnp.concatenate(parts, 0)


def edge_rows(tracer, north_wind, position, band_count, with_wind, rider=None):
    row_count = tracer.shape[3]
    width_cells = tracer.shape[4]
    top = [tracer[:, :, 0::2, row_count - 3 :, :].reshape(-1, width_cells)]
    low = [tracer[:, :, 1::2, 0:3, :].reshape(-1, width_cells)]
    if with_wind:
        top.append(north_wind[:, 0::2, row_count - 1, :].reshape(-1, width_cells))
        low.append(north_wind[:, 1::2, 0, :].reshape(-1, width_cells))
    top = jnp.concatenate(top, 0)
    low = jnp.concatenate(low, 0)
    send = jnp.where(position == band_count - 1, top, jnp.where(position == 0, low, 0.0))
    send = jnp.flip(send.T, 0).reshape(band_count, -1)
    width = send.shape[1]
    if rider is not None:
        send = jnp.concatenate([send, rider.astype(send.dtype)], 1)
    got = lax.all_to_all(send, "space", 0, 0, tiled=True)
    count = top.shape[0]
    rode = got[:, width:]
    got = got[:, :width]
    return got[band_count - 1].reshape(-1, count), got[0].reshape(-1, count), rode


def column_halos(
    tracer, east_wind, north_wind, position, band_count, edge_wind, faces_known, rider=None
):
    scenarios, levels, _, row_count, width_cells = tracer.shape
    top, low, rode = edge_rows(tracer, north_wind, position, band_count, edge_wind is None, rider)
    cells = scenarios * levels * 3 * 3
    top_layers = top[:, :cells].reshape(row_count, scenarios, levels, 3, 3)
    low_layers = low[:, :cells].reshape(row_count, scenarios, levels, 3, 3)
    if edge_wind is None:
        edge_wind = (
            top[:, cells:].reshape(row_count, levels, 3),
            low[:, cells:].reshape(row_count, levels, 3),
        )
    top_wind, low_wind = edge_wind
    west_faces, east_faces, west_speeds, east_speeds = [], [], [], []
    for face_number in range(6):
        half = face_number // 2
        if face_number % 2 == 0:
            west_cells = jnp.moveaxis(top_layers[:, :, :, (half - 1) % 3], 0, 2)
            west_speed = top_wind[:, :, (half - 1) % 3].T
            east_cells = tracer[:, :, (face_number + 1) % 6, :, 0:3]
            east_speed = east_wind[:, (face_number + 1) % 6, :, 0]
        else:
            west_cells = tracer[:, :, (face_number - 1) % 6, :, width_cells - 3 :]
            west_speed = east_wind[:, (face_number - 1) % 6, :, width_cells - 1]
            east_cells = jnp.moveaxis(low_layers[:, :, :, (half + 1) % 3], 0, 2)
            east_speed = low_wind[:, :, (half + 1) % 3].T
        west_faces.append(west_cells)
        east_faces.append(east_cells)
        west_speeds.append(west_speed)
        east_speeds.append(east_speed)
    padded = jnp.concatenate(
        [jnp.stack(west_faces, 2), tracer, jnp.stack(east_faces, 2)], -1
    )
    if faces_known is None:
        speeds = jnp.concatenate(
            [
                jnp.stack(west_speeds, 1)[..., None],
                east_wind,
                jnp.stack(east_speeds, 1)[..., None],
            ],
            -1,
        )
        faces_known = 0.5 * (speeds[..., :-1] + speeds[..., 1:])
    return (padded, faces_known, edge_wind, rode)


def edge_columns(tracer, east_wind, position, band_count, with_wind):
    scenarios, levels, _, row_count, width_cells = tracer.shape
    to_top = [jnp.moveaxis(tracer[:, :, 0::2, :, 0:3], 3, 0).reshape(row_count, -1)]
    to_low = [jnp.moveaxis(tracer[:, :, 1::2, :, width_cells - 3 :], 3, 0).reshape(row_count, -1)]
    if with_wind:
        to_top.append(jnp.moveaxis(east_wind[:, 0::2, :, 0], 2, 0).reshape(row_count, -1))
        to_low.append(
            jnp.moveaxis(east_wind[:, 1::2, :, width_cells - 1], 2, 0).reshape(row_count, -1)
        )
    to_top = jnp.concatenate(to_top, 1)
    to_low = jnp.concatenate(to_low, 1)
    count = to_top.shape[1]
    destination = lax.broadcasted_iota(jnp.int32, (band_count, row_count, count), 0)
    send = jnp.where(
        destination == band_count - 1, to_top[None], jnp.where(destination == 0, to_low[None], 0.0)
    ).astype(to_top.dtype)
    got = lax.all_to_all(send, "space", 0, 0, tiled=True)
    flipped = jnp.flip(got.reshape(-1, count), 0).T
    cells = scenarios * levels * 3 * 3
    layers = flipped[:cells].reshape(scenarios, levels, 3, 3, band_count * row_count)
    wind = None
    if with_wind:
        wind = flipped[cells:].reshape(levels, 3, band_count * row_count)
    return layers, wind


def row_halos(tracer, east_wind, north_wind, position, band_count, row_wind, faces_known):
    first_step = row_wind is None
    shifted = []
    for step_by, lowest in ((-1, True), (1, False)):
        packed = pack_rows(tracer, north_wind if first_step else None, lowest)
        shifted.append(from_behind(packed, "space", step_by))
    edge_layers, edge_speed = edge_columns(tracer, east_wind, position, band_count, first_step)
    layer_rows = tracer.shape[0] * tracer.shape[1] * 18
    width_cells = tracer.shape[4]
    if first_step:
        levels = tracer.shape[1]
        row_wind = tuple(
            packed[layer_rows:].reshape(levels, 6, width_cells) for packed in shifted
        ) + (edge_speed,)
    above_wind, below_wind, edge_speed = row_wind
    above_layers, below_layers = (
        packed[:layer_rows].reshape(tracer.shape[0], tracer.shape[1], 6, 3, width_cells)
        for packed in shifted
    )
    at_top = position == band_count - 1
    at_bottom = position == 0
    south_faces, north_faces, south_speeds, north_speeds = [], [], [], []
    for face_number in range(6):
        half = face_number // 2
        if face_number % 2 == 0:
            north_cells = jnp.where(
                at_top,
                edge_layers[:, :, (half + 1) % 3],
                above_layers[:, :, face_number],
            )
            north_speed = jnp.where(
                at_top,
                edge_speed[:, (half + 1) % 3],
                above_wind[:, face_number],
            )
            south_cells = jnp.where(
                at_bottom,
                below_layers[:, :, (face_number - 1) % 6],
                below_layers[:, :, face_number],
            )
            south_speed = jnp.where(
                at_bottom, below_wind[:, (face_number - 1) % 6], below_wind[:, face_number]
            )
        else:
            north_cells = jnp.where(
                at_top, above_layers[:, :, (face_number + 1) % 6], above_layers[:, :, face_number]
            )
            north_speed = jnp.where(
                at_top, above_wind[:, (face_number + 1) % 6], above_wind[:, face_number]
            )
            south_cells = jnp.where(
                at_bottom,
                edge_layers[:, :, (half - 1) % 3],
                below_layers[:, :, face_number],
            )
            south_speed = jnp.where(
                at_bottom,
                edge_speed[:, (half - 1) % 3],
                below_wind[:, face_number],
            )
        south_faces.append(south_cells)
        north_faces.append(north_cells)
        south_speeds.append(south_speed)
        north_speeds.append(north_speed)
    padded = jnp.concatenate(
        [jnp.stack(south_faces, 2), tracer, jnp.stack(north_faces, 2)], -2
    )
    if faces_known is None:
        speeds = jnp.concatenate(
            [
                jnp.stack(south_speeds, 1)[:, :, None, :],
                north_wind,
                jnp.stack(north_speeds, 1)[:, :, None, :],
            ],
            -2,
        )
        faces_known = 0.5 * (speeds[:, :, :-1, :] + speeds[:, :, 1:, :])
    return (padded, faces_known, row_wind)


def slot_plan(tile_target, band_count):
    target_band = tile_target // TGT_DEV
    target_block = tile_target % TGT_DEV
    band_hot = (target_band[:, None] == jnp.arange(band_count)[None, :]).astype(jnp.int32)
    rank = jnp.sum((jnp.cumsum(band_hot, 0) - band_hot) * band_hot, 1)
    slot = jnp.where(rank < SLOTS, target_band * SLOTS + rank, -1)
    slot_hot = (slot[None, :] == jnp.arange(band_count * SLOTS)[:, None]).astype(jnp.float32)
    slot_block = jnp.sum(slot_hot * target_block[None, :].astype(jnp.float32), 1)
    return slot_hot, slot_block.reshape(band_count, SLOTS)


def regrid(tracer, tile_source, slot_hot, got_block, intersection, band_count):
    scenarios = tracer.shape[0]
    levels = tracer.shape[1]
    batch_rows = scenarios * levels
    block_cells = intersection.shape[1]
    blocks = tracer.astype(jnp.bfloat16).reshape(batch_rows, -1, block_cells)
    chosen = jnp.take(blocks, tile_source, axis=1)
    partial_value = jnp.einsum(
        "btk,tkc->tbc", chosen, intersection, preferred_element_type=jnp.float32
    )
    slotted = jnp.einsum(
        "st,tbc->sbc", slot_hot, partial_value, precision=lax.Precision.HIGHEST
    )
    send = slotted.reshape(band_count, SLOTS * batch_rows, block_cells)
    got = lax.all_to_all(send, "space", 0, 0, tiled=True)
    values = got.reshape(band_count * SLOTS, batch_rows, block_cells)
    block_hot = (
        got_block.reshape(-1)[None, :] == jnp.arange(TGT_DEV)[:, None].astype(jnp.float32)
    ).astype(jnp.float32)
    summed = jnp.einsum("ks,sbc->bkc", block_hot, values, precision=lax.Precision.HIGHEST)
    return summed.reshape(scenarios, levels, TGT_DEV, block_cells)


def moments_of(regridded):
    scenarios = regridded.shape[0]
    scen_count = lax.axis_size("scen")
    copies = jnp.broadcast_to(regridded, (scen_count,) + regridded.shape[1:])
    everyone = lax.all_to_all(copies, "scen", 0, 0, tiled=True)
    moment_sums = jnp.stack([jnp.sum(everyone, 0), jnp.sum(everyone * everyone, 0)])
    return moment_sums / (scenarios * scen_count)


def local(concentration, emissions, courant, tile_source, tile_target, intersection):
    band_count = lax.axis_size("space")
    position = lax.axis_index("space")
    tracer = concentration.at[:, 0].add(emissions)
    east_wind = courant[0]
    north_wind = courant[1]
    edge_wind = None
    row_wind = None
    cx = None
    cy = None
    slot_hot, slot_block = slot_plan(tile_target, band_count)
    got_block = None
    for step_number in range(2):
        padded, cx, edge_wind, rode = column_halos(
            tracer,
            east_wind,
            north_wind,
            position,
            band_count,
            edge_wind,
            cx,
            slot_block if step_number == 0 else None,
        )
        if step_number == 0:
            got_block = rode
        tracer = parabola_sweep(padded, cx, 4)
        padded, cy, row_wind = row_halos(
            tracer, east_wind, north_wind, position, band_count, row_wind, cy
        )
        tracer = parabola_sweep(padded, cy, 3)
    regridded = regrid(tracer, tile_source, slot_hot, got_block, intersection, band_count)
    ensemble_moments = moments_of(regridded)
    return (tracer, regridded, ensemble_moments)


def solution(mesh):
    return jax.shard_map(
        local,
        mesh=mesh,
        in_specs=(
            P("scen", None, None, "space", None),
            P("scen", None, "space", None),
            P(None, None, None, "space", None),
            P("space"),
            P("space"),
            P("space", None, None),
        ),
        out_specs=(
            P("scen", None, None, "space", None),
            P("scen", None, "space", None),
            P(None, None, "space", None),
        ),
        check_vma=False,
    )
```

```python
import jax
import jax.numpy as jnp
from jax import lax
from jax.sharding import PartitionSpec as P

TGT_DEV = 32
SLOTS = 16


def from_behind(block, axis, distance):
    devices = range(lax.axis_size(axis))
    route = [((i - distance) % len(devices), i) for i in devices]
    return lax.ppermute(block, axis, route)


def parabola_sweep(padded, courant_faces, sweep_axis):
    cells_along = padded.shape[sweep_axis] - 6

    def window(values_in, first_cell, length):
        return lax.slice_in_dim(values_in, first_cell, first_cell + length, axis=sweep_axis)

    edge_values = 7.0 / 12.0 * (
        window(padded, 1, cells_along + 3) + window(padded, 2, cells_along + 3)
    ) - 1.0 / 12.0 * (window(padded, 0, cells_along + 3) + window(padded, 3, cells_along + 3))
    left_edge = window(edge_values, 0, cells_along + 2)
    right_edge = window(edge_values, 1, cells_along + 2)
    centre = window(padded, 2, cells_along + 2)
    slopes = right_edge - left_edge
    curvature = 6.0 * centre - 3.0 * (left_edge + right_edge)
    backward = -courant_faces
    upwind_left = courant_faces * (
        window(right_edge, 0, cells_along + 1)
        - 0.5
        * courant_faces
        * (
            window(slopes, 0, cells_along + 1)
            - (1.0 - 2.0 * courant_faces / 3.0) * window(curvature, 0, cells_along + 1)
        )
    )
    upwind_right = courant_faces * (
        window(left_edge, 1, cells_along + 1)
        + 0.5
        * backward
        * (
            window(slopes, 1, cells_along + 1)
            + (1.0 - 2.0 * backward / 3.0) * window(curvature, 1, cells_along + 1)
        )
    )
    fluxes = jnp.where(courant_faces >= 0.0, upwind_left, upwind_right)
    return window(padded, 3, cells_along) - (
        window(fluxes, 1, cells_along) - window(fluxes, 0, cells_along)
    )


def pack_rows(tracer, north_wind, lowest):
    row_count = tracer.shape[3]
    width_cells = tracer.shape[4]
    if lowest:
        layers = tracer[:, :, :, 0:3, :]
    else:
        layers = tracer[:, :, :, row_count - 3 :, :]
    parts = [layers.reshape(-1, width_cells)]
    if north_wind is not None:
        wind_row = north_wind[:, :, 0:1, :] if lowest else north_wind[:, :, row_count - 1 :, :]
        parts.append(wind_row.reshape(-1, width_cells))
    return jnp.concatenate(parts, 0)


def edge_rows(tracer, north_wind, position, band_count, with_wind, rider=None):
    row_count = tracer.shape[3]
    width_cells = tracer.shape[4]
    top = [tracer[:, :, 0::2, row_count - 3 :, :].reshape(-1, width_cells)]
    low = [tracer[:, :, 1::2, 0:3, :].reshape(-1, width_cells)]
    if with_wind:
        top.append(north_wind[:, 0::2, row_count - 1, :].reshape(-1, width_cells))
        low.append(north_wind[:, 1::2, 0, :].reshape(-1, width_cells))
    top = jnp.concatenate(top, 0)
    low = jnp.concatenate(low, 0)
    send = jnp.where(position == band_count - 1, top, jnp.where(position == 0, low, 0.0))
    send = jnp.flip(send.T, 0).reshape(band_count, -1)
    width = send.shape[1]
    if rider is not None:
        send = jnp.concatenate([send, rider.astype(send.dtype)], 1)
    got = lax.all_to_all(send, "space", 0, 0, tiled=True)
    count = top.shape[0]
    rode = got[:, width:]
    got = got[:, :width]
    return got[band_count - 1].reshape(-1, count), got[0].reshape(-1, count), rode


def column_halos(
    tracer, east_wind, north_wind, position, band_count, edge_wind, faces_known, rider=None
):
    scenarios, levels, _, row_count, width_cells = tracer.shape
    top, low, rode = edge_rows(tracer, north_wind, position, band_count, edge_wind is None, rider)
    cells = scenarios * levels * 3 * 3
    top_layers = top[:, :cells].reshape(row_count, scenarios, levels, 3, 3)
    low_layers = low[:, :cells].reshape(row_count, scenarios, levels, 3, 3)
    if edge_wind is None:
        edge_wind = (
            top[:, cells:].reshape(row_count, levels, 3),
            low[:, cells:].reshape(row_count, levels, 3),
        )
    top_wind, low_wind = edge_wind
    west_faces, east_faces, west_speeds, east_speeds = [], [], [], []
    for face_number in range(6):
        half = face_number // 2
        if face_number % 2 == 0:
            west_cells = jnp.moveaxis(top_layers[:, :, :, (half - 1) % 3], 0, 2)
            west_speed = top_wind[:, :, (half - 1) % 3].T
            east_cells = tracer[:, :, (face_number + 1) % 6, :, 0:3]
            east_speed = east_wind[:, (face_number + 1) % 6, :, 0]
        else:
            west_cells = tracer[:, :, (face_number - 1) % 6, :, width_cells - 3 :]
            west_speed = east_wind[:, (face_number - 1) % 6, :, width_cells - 1]
            east_cells = jnp.moveaxis(low_layers[:, :, :, (half + 1) % 3], 0, 2)
            east_speed = low_wind[:, :, (half + 1) % 3].T
        west_faces.append(west_cells)
        east_faces.append(east_cells)
        west_speeds.append(west_speed)
        east_speeds.append(east_speed)
    padded = jnp.concatenate(
        [jnp.stack(west_faces, 2), tracer, jnp.stack(east_faces, 2)], -1
    )
    if faces_known is None:
        speeds = jnp.concatenate(
            [
                jnp.stack(west_speeds, 1)[..., None],
                east_wind,
                jnp.stack(east_speeds, 1)[..., None],
            ],
            -1,
        )
        faces_known = 0.5 * (speeds[..., :-1] + speeds[..., 1:])
    return (padded, faces_known, edge_wind, rode)


def edge_columns(tracer, east_wind, position, band_count, with_wind, rider=None):
    scenarios, levels, _, row_count, width_cells = tracer.shape
    to_top = [jnp.moveaxis(tracer[:, :, 0::2, :, 0:3], 3, 0).reshape(row_count, -1)]
    to_low = [jnp.moveaxis(tracer[:, :, 1::2, :, width_cells - 3 :], 3, 0).reshape(row_count, -1)]
    if with_wind:
        to_top.append(jnp.moveaxis(east_wind[:, 0::2, :, 0], 2, 0).reshape(row_count, -1))
        to_low.append(
            jnp.moveaxis(east_wind[:, 1::2, :, width_cells - 1], 2, 0).reshape(row_count, -1)
        )
    to_top = jnp.concatenate(to_top, 1)
    to_low = jnp.concatenate(to_low, 1)
    count = to_top.shape[1]
    destination = lax.broadcasted_iota(jnp.int32, (band_count, row_count, count), 0)
    send = jnp.where(
        destination == band_count - 1, to_top[None], jnp.where(destination == 0, to_low[None], 0.0)
    ).astype(to_top.dtype)
    rode = None
    if rider is not None:
        send = jnp.concatenate([send.reshape(band_count, -1), rider.astype(send.dtype)], 1)
    got = lax.all_to_all(send, "space", 0, 0, tiled=True)
    if rider is not None:
        rode = got[:, row_count * count :]
        got = got[:, : row_count * count].reshape(band_count, row_count, count)
    flipped = jnp.flip(got.reshape(-1, count), 0).T
    cells = scenarios * levels * 3 * 3
    layers = flipped[:cells].reshape(scenarios, levels, 3, 3, band_count * row_count)
    wind = None
    if with_wind:
        wind = flipped[cells:].reshape(levels, 3, band_count * row_count)
    return layers, wind, rode


def row_halos(
    tracer, east_wind, north_wind, position, band_count, row_wind, faces_known, rider=None
):
    first_step = row_wind is None
    shifted = []
    for step_by, lowest in ((-1, True), (1, False)):
        packed = pack_rows(tracer, north_wind if first_step else None, lowest)
        shifted.append(from_behind(packed, "space", step_by))
    edge_layers, edge_speed, rode = edge_columns(
        tracer, east_wind, position, band_count, first_step, rider
    )
    layer_rows = tracer.shape[0] * tracer.shape[1] * 18
    width_cells = tracer.shape[4]
    if first_step:
        levels = tracer.shape[1]
        row_wind = tuple(
            packed[layer_rows:].reshape(levels, 6, width_cells) for packed in shifted
        ) + (edge_speed,)
    above_wind, below_wind, edge_speed = row_wind
    above_layers, below_layers = (
        packed[:layer_rows].reshape(tracer.shape[0], tracer.shape[1], 6, 3, width_cells)
        for packed in shifted
    )
    at_top = position == band_count - 1
    at_bottom = position == 0
    south_faces, north_faces, south_speeds, north_speeds = [], [], [], []
    for face_number in range(6):
        half = face_number // 2
        if face_number % 2 == 0:
            north_cells = jnp.where(
                at_top,
                edge_layers[:, :, (half + 1) % 3],
                above_layers[:, :, face_number],
            )
            north_speed = jnp.where(
                at_top,
                edge_speed[:, (half + 1) % 3],
                above_wind[:, face_number],
            )
            south_cells = jnp.where(
                at_bottom,
                below_layers[:, :, (face_number - 1) % 6],
                below_layers[:, :, face_number],
            )
            south_speed = jnp.where(
                at_bottom, below_wind[:, (face_number - 1) % 6], below_wind[:, face_number]
            )
        else:
            north_cells = jnp.where(
                at_top, above_layers[:, :, (face_number + 1) % 6], above_layers[:, :, face_number]
            )
            north_speed = jnp.where(
                at_top, above_wind[:, (face_number + 1) % 6], above_wind[:, face_number]
            )
            south_cells = jnp.where(
                at_bottom,
                edge_layers[:, :, (half - 1) % 3],
                below_layers[:, :, face_number],
            )
            south_speed = jnp.where(
                at_bottom,
                edge_speed[:, (half - 1) % 3],
                below_wind[:, face_number],
            )
        south_faces.append(south_cells)
        north_faces.append(north_cells)
        south_speeds.append(south_speed)
        north_speeds.append(north_speed)
    padded = jnp.concatenate(
        [jnp.stack(south_faces, 2), tracer, jnp.stack(north_faces, 2)], -2
    )
    if faces_known is None:
        speeds = jnp.concatenate(
            [
                jnp.stack(south_speeds, 1)[:, :, None, :],
                north_wind,
                jnp.stack(north_speeds, 1)[:, :, None, :],
            ],
            -2,
        )
        faces_known = 0.5 * (speeds[:, :, :-1, :] + speeds[:, :, 1:, :])
    return (padded, faces_known, row_wind, rode)


def slot_plan(tile_target, band_count):
    target_band = tile_target // TGT_DEV
    target_block = tile_target % TGT_DEV
    band_hot = (target_band[:, None] == jnp.arange(band_count)[None, :]).astype(jnp.int32)
    rank = jnp.sum((jnp.cumsum(band_hot, 0) - band_hot) * band_hot, 1)
    slot = jnp.where(rank < SLOTS, target_band * SLOTS + rank, -1)
    slot_hot = (slot[None, :] == jnp.arange(band_count * SLOTS)[:, None]).astype(jnp.float32)
    slot_block = jnp.sum(slot_hot * target_block[None, :].astype(jnp.float32), 1)
    return slot_hot, slot_block.reshape(band_count, SLOTS)


def regrid(tracer, tile_source, slot_hot, got_block, intersection, band_count):
    scenarios = tracer.shape[0]
    levels = tracer.shape[1]
    batch_rows = scenarios * levels
    block_cells = intersection.shape[1]
    blocks = tracer.astype(jnp.bfloat16).reshape(batch_rows, -1, block_cells)
    chosen = jnp.take(blocks, tile_source, axis=1)
    partial_value = jnp.einsum(
        "btk,tkc->tbc", chosen, intersection, preferred_element_type=jnp.float32
    )
    slotted = jnp.einsum(
        "st,tbc->sbc", slot_hot, partial_value, precision=lax.Precision.HIGHEST
    )
    send = slotted.reshape(band_count, SLOTS * batch_rows, block_cells)
    got = lax.all_to_all(send, "space", 0, 0, tiled=True)
    values = got.reshape(band_count * SLOTS, batch_rows, block_cells)
    block_hot = (
        got_block.reshape(-1)[None, :] == jnp.arange(TGT_DEV)[:, None].astype(jnp.float32)
    ).astype(jnp.float32)
    summed = jnp.einsum("ks,sbc->bkc", block_hot, values, precision=lax.Precision.HIGHEST)
    return summed.reshape(scenarios, levels, TGT_DEV, block_cells)


def moments_of(regridded):
    scenarios = regridded.shape[0]
    scen_count = lax.axis_size("scen")
    copies = jnp.broadcast_to(regridded, (scen_count,) + regridded.shape[1:])
    everyone = lax.all_to_all(copies, "scen", 0, 0, tiled=True)
    moment_sums = jnp.stack([jnp.sum(everyone, 0), jnp.sum(everyone * everyone, 0)])
    return moment_sums / (scenarios * scen_count)


def local(concentration, emissions, courant, tile_source, tile_target, intersection):
    band_count = lax.axis_size("space")
    position = lax.axis_index("space")
    tracer = concentration.at[:, 0].add(emissions)
    east_wind = courant[0]
    north_wind = courant[1]
    edge_wind = None
    row_wind = None
    cx = None
    cy = None
    slot_hot, slot_block = slot_plan(tile_target, band_count)
    got_block = None
    for step_number in range(2):
        padded, cx, edge_wind, rode = column_halos(
            tracer,
            east_wind,
            north_wind,
            position,
            band_count,
            edge_wind,
            cx,
        )
        tracer = parabola_sweep(padded, cx, 4)
        padded, cy, row_wind, rode = row_halos(
            tracer,
            east_wind,
            north_wind,
            position,
            band_count,
            row_wind,
            cy,
            slot_block if step_number == 1 else None,
        )
        if step_number == 1:
            got_block = rode
        tracer = parabola_sweep(padded, cy, 3)
    regridded = regrid(tracer, tile_source, slot_hot, got_block, intersection, band_count)
    ensemble_moments = moments_of(regridded)
    return (tracer, regridded, ensemble_moments)


def solution(mesh):
    return jax.shard_map(
        local,
        mesh=mesh,
        in_specs=(
            P("scen", None, None, "space", None),
            P("scen", None, "space", None),
            P(None, None, None, "space", None),
            P("space"),
            P("space"),
            P("space", None, None),
        ),
        out_specs=(
            P("scen", None, None, "space", None),
            P("scen", None, "space", None),
            P(None, None, "space", None),
        ),
        check_vma=False,
    )
```

```python
import jax
import jax.numpy as jnp
from jax import lax
from jax.sharding import PartitionSpec as P

TGT_DEV = 32
SLOTS = 16


def from_behind(block, axis, distance):
    devices = range(lax.axis_size(axis))
    route = [((i - distance) % len(devices), i) for i in devices]
    return lax.ppermute(block, axis, route)


def parabola_sweep(padded, courant_faces, sweep_axis):
    cells_along = padded.shape[sweep_axis] - 6

    def window(values_in, first_cell, length):
        return lax.slice_in_dim(values_in, first_cell, first_cell + length, axis=sweep_axis)

    edge_values = 7.0 / 12.0 * (
        window(padded, 1, cells_along + 3) + window(padded, 2, cells_along + 3)
    ) - 1.0 / 12.0 * (window(padded, 0, cells_along + 3) + window(padded, 3, cells_along + 3))
    left_edge = window(edge_values, 0, cells_along + 2)
    right_edge = window(edge_values, 1, cells_along + 2)
    centre = window(padded, 2, cells_along + 2)
    slopes = right_edge - left_edge
    curvature = 6.0 * centre - 3.0 * (left_edge + right_edge)
    backward = -courant_faces
    upwind_left = courant_faces * (
        window(right_edge, 0, cells_along + 1)
        - 0.5
        * courant_faces
        * (
            window(slopes, 0, cells_along + 1)
            - (1.0 - 2.0 * courant_faces / 3.0) * window(curvature, 0, cells_along + 1)
        )
    )
    upwind_right = courant_faces * (
        window(left_edge, 1, cells_along + 1)
        + 0.5
        * backward
        * (
            window(slopes, 1, cells_along + 1)
            + (1.0 - 2.0 * backward / 3.0) * window(curvature, 1, cells_along + 1)
        )
    )
    fluxes = jnp.where(courant_faces >= 0.0, upwind_left, upwind_right)
    return window(padded, 3, cells_along) - (
        window(fluxes, 1, cells_along) - window(fluxes, 0, cells_along)
    )


def pack_rows(tracer, north_wind, lowest):
    row_count = tracer.shape[3]
    width_cells = tracer.shape[4]
    if lowest:
        layers = tracer[:, :, :, 0:3, :]
    else:
        layers = tracer[:, :, :, row_count - 3 :, :]
    parts = [layers.reshape(-1, width_cells)]
    if north_wind is not None:
        wind_row = north_wind[:, :, 0:1, :] if lowest else north_wind[:, :, row_count - 1 :, :]
        parts.append(wind_row.reshape(-1, width_cells))
    return jnp.concatenate(parts, 0)


def edge_rows(tracer, north_wind, position, band_count, with_wind, rider=None):
    row_count = tracer.shape[3]
    width_cells = tracer.shape[4]
    top = [tracer[:, :, 0::2, row_count - 3 :, :].reshape(-1, width_cells)]
    low = [tracer[:, :, 1::2, 0:3, :].reshape(-1, width_cells)]
    if with_wind:
        top.append(north_wind[:, 0::2, row_count - 1, :].reshape(-1, width_cells))
        low.append(north_wind[:, 1::2, 0, :].reshape(-1, width_cells))
    top = jnp.concatenate(top, 0)
    low = jnp.concatenate(low, 0)
    send = jnp.where(position == band_count - 1, top, jnp.where(position == 0, low, 0.0))
    send = jnp.flip(send.T, 0).reshape(band_count, -1)
    width = send.shape[1]
    if rider is not None:
        send = jnp.concatenate([send, rider.astype(send.dtype)], 1)
    got = lax.all_to_all(send, "space", 0, 0, tiled=True)
    count = top.shape[0]
    rode = got[:, width:]
    got = got[:, :width]
    return got[band_count - 1].reshape(-1, count), got[0].reshape(-1, count), rode


def column_halos(
    tracer, east_wind, north_wind, position, band_count, edge_wind, faces_known, rider=None
):
    scenarios, levels, _, row_count, width_cells = tracer.shape
    top, low, rode = edge_rows(tracer, north_wind, position, band_count, edge_wind is None, rider)
    cells = scenarios * levels * 3 * 3
    top_layers = top[:, :cells].reshape(row_count, scenarios, levels, 3, 3)
    low_layers = low[:, :cells].reshape(row_count, scenarios, levels, 3, 3)
    if edge_wind is None:
        edge_wind = (
            top[:, cells:].reshape(row_count, levels, 3),
            low[:, cells:].reshape(row_count, levels, 3),
        )
    top_wind, low_wind = edge_wind
    west_faces, east_faces, west_speeds, east_speeds = [], [], [], []
    for face_number in range(6):
        half = face_number // 2
        if face_number % 2 == 0:
            west_cells = jnp.moveaxis(top_layers[:, :, :, (half - 1) % 3], 0, 2)
            west_speed = top_wind[:, :, (half - 1) % 3].T
            east_cells = tracer[:, :, (face_number + 1) % 6, :, 0:3]
            east_speed = east_wind[:, (face_number + 1) % 6, :, 0]
        else:
            west_cells = tracer[:, :, (face_number - 1) % 6, :, width_cells - 3 :]
            west_speed = east_wind[:, (face_number - 1) % 6, :, width_cells - 1]
            east_cells = jnp.moveaxis(low_layers[:, :, :, (half + 1) % 3], 0, 2)
            east_speed = low_wind[:, :, (half + 1) % 3].T
        west_faces.append(west_cells)
        east_faces.append(east_cells)
        west_speeds.append(west_speed)
        east_speeds.append(east_speed)
    padded = jnp.concatenate(
        [jnp.stack(west_faces, 2), tracer, jnp.stack(east_faces, 2)], -1
    )
    if faces_known is None:
        speeds = jnp.concatenate(
            [
                jnp.stack(west_speeds, 1)[..., None],
                east_wind,
                jnp.stack(east_speeds, 1)[..., None],
            ],
            -1,
        )
        faces_known = 0.5 * (speeds[..., :-1] + speeds[..., 1:])
    return (padded, faces_known, edge_wind, rode)


def edge_columns(tracer, east_wind, position, band_count, with_wind, rider=None):
    scenarios, levels, _, row_count, width_cells = tracer.shape
    to_top = [jnp.moveaxis(tracer[:, :, 0::2, :, 0:3], 3, 0).reshape(row_count, -1)]
    to_low = [jnp.moveaxis(tracer[:, :, 1::2, :, width_cells - 3 :], 3, 0).reshape(row_count, -1)]
    if with_wind:
        to_top.append(jnp.moveaxis(east_wind[:, 0::2, :, 0], 2, 0).reshape(row_count, -1))
        to_low.append(
            jnp.moveaxis(east_wind[:, 1::2, :, width_cells - 1], 2, 0).reshape(row_count, -1)
        )
    to_top = jnp.concatenate(to_top, 1)
    to_low = jnp.concatenate(to_low, 1)
    count = to_top.shape[1]
    destination = lax.broadcasted_iota(jnp.int32, (band_count, row_count, count), 0)
    send = jnp.where(
        destination == band_count - 1, to_top[None], jnp.where(destination == 0, to_low[None], 0.0)
    ).astype(to_top.dtype)
    rode = None
    if rider is not None:
        send = jnp.concatenate([send.reshape(band_count, -1), rider.astype(send.dtype)], 1)
    got = lax.all_to_all(send, "space", 0, 0, tiled=True)
    if rider is not None:
        rode = got[:, row_count * count :]
        got = got[:, : row_count * count].reshape(band_count, row_count, count)
    flipped = jnp.flip(got.reshape(-1, count), 0).T
    cells = scenarios * levels * 3 * 3
    layers = flipped[:cells].reshape(scenarios, levels, 3, 3, band_count * row_count)
    wind = None
    if with_wind:
        wind = flipped[cells:].reshape(levels, 3, band_count * row_count)
    return layers, wind, rode


def row_halos(
    tracer, east_wind, north_wind, position, band_count, row_wind, faces_known, rider=None
):
    first_step = row_wind is None
    shifted = []
    for step_by, lowest in ((-1, True), (1, False)):
        packed = pack_rows(tracer, north_wind if first_step else None, lowest)
        shifted.append(from_behind(packed, "space", step_by))
    edge_layers, edge_speed, rode = edge_columns(
        tracer, east_wind, position, band_count, first_step, rider
    )
    layer_rows = tracer.shape[0] * tracer.shape[1] * 18
    width_cells = tracer.shape[4]
    if first_step:
        levels = tracer.shape[1]
        row_wind = tuple(
            packed[layer_rows:].reshape(levels, 6, width_cells) for packed in shifted
        ) + (edge_speed,)
    above_wind, below_wind, edge_speed = row_wind
    above_layers, below_layers = (
        packed[:layer_rows].reshape(tracer.shape[0], tracer.shape[1], 6, 3, width_cells)
        for packed in shifted
    )
    at_top = position == band_count - 1
    at_bottom = position == 0
    south_faces, north_faces, south_speeds, north_speeds = [], [], [], []
    for face_number in range(6):
        half = face_number // 2
        if face_number % 2 == 0:
            north_cells = jnp.where(
                at_top,
                edge_layers[:, :, (half + 1) % 3],
                above_layers[:, :, face_number],
            )
            north_speed = jnp.where(
                at_top,
                edge_speed[:, (half + 1) % 3],
                above_wind[:, face_number],
            )
            south_cells = jnp.where(
                at_bottom,
                below_layers[:, :, (face_number - 1) % 6],
                below_layers[:, :, face_number],
            )
            south_speed = jnp.where(
                at_bottom, below_wind[:, (face_number - 1) % 6], below_wind[:, face_number]
            )
        else:
            north_cells = jnp.where(
                at_top, above_layers[:, :, (face_number + 1) % 6], above_layers[:, :, face_number]
            )
            north_speed = jnp.where(
                at_top, above_wind[:, (face_number + 1) % 6], above_wind[:, face_number]
            )
            south_cells = jnp.where(
                at_bottom,
                edge_layers[:, :, (half - 1) % 3],
                below_layers[:, :, face_number],
            )
            south_speed = jnp.where(
                at_bottom,
                edge_speed[:, (half - 1) % 3],
                below_wind[:, face_number],
            )
        south_faces.append(south_cells)
        north_faces.append(north_cells)
        south_speeds.append(south_speed)
        north_speeds.append(north_speed)
    padded = jnp.concatenate(
        [jnp.stack(south_faces, 2), tracer, jnp.stack(north_faces, 2)], -2
    )
    if faces_known is None:
        speeds = jnp.concatenate(
            [
                jnp.stack(south_speeds, 1)[:, :, None, :],
                north_wind,
                jnp.stack(north_speeds, 1)[:, :, None, :],
            ],
            -2,
        )
        faces_known = 0.5 * (speeds[:, :, :-1, :] + speeds[:, :, 1:, :])
    return (padded, faces_known, row_wind, rode)


def slot_plan(tile_target, band_count):
    target_band = tile_target // TGT_DEV
    target_block = tile_target % TGT_DEV
    band_hot = (target_band[:, None] == jnp.arange(band_count)[None, :]).astype(jnp.int32)
    rank = jnp.sum((jnp.cumsum(band_hot, 0) - band_hot) * band_hot, 1)
    slot = jnp.where(rank < SLOTS, target_band * SLOTS + rank, -1)
    slot_hot = (slot[None, :] == jnp.arange(band_count * SLOTS)[:, None]).astype(jnp.float32)
    slot_block = jnp.sum(slot_hot * target_block[None, :].astype(jnp.float32), 1)
    return slot_hot, slot_block.reshape(band_count, SLOTS)


def regrid(tracer, tile_source, slot_hot, got_block, intersection, band_count):
    scenarios = tracer.shape[0]
    levels = tracer.shape[1]
    batch_rows = scenarios * levels
    block_cells = intersection.shape[1]
    blocks = tracer.astype(jnp.bfloat16).reshape(batch_rows, -1, block_cells)
    chosen = jnp.take(blocks, tile_source, axis=1)
    partial_value = jnp.einsum(
        "btk,tkc->tbc", chosen, intersection, preferred_element_type=jnp.float32
    )
    slotted = jnp.einsum(
        "st,tbc->sbc", slot_hot, partial_value, precision=lax.Precision.HIGHEST
    )
    send = slotted.reshape(band_count, SLOTS * batch_rows, block_cells)
    got = lax.all_to_all(send, "space", 0, 0, tiled=True)
    values = got.reshape(band_count * SLOTS, batch_rows, block_cells)
    block_hot = (
        got_block.reshape(-1)[None, :] == jnp.arange(TGT_DEV)[:, None].astype(jnp.float32)
    ).astype(jnp.float32)
    summed = jnp.einsum("ks,sbc->bkc", block_hot, values, precision=lax.Precision.HIGHEST)
    return summed.reshape(scenarios, levels, TGT_DEV, block_cells)


def moments_of(regridded):
    scenarios = regridded.shape[0]
    scen_count = lax.axis_size("scen")
    copies = jnp.broadcast_to(regridded, (scen_count,) + regridded.shape[1:])
    everyone = lax.all_to_all(copies, "scen", 0, 0, tiled=True)
    moment_sums = jnp.stack([jnp.sum(everyone, 0), jnp.sum(everyone * everyone, 0)])
    return moment_sums / (scenarios * scen_count)


def local(concentration, emissions, courant, tile_source, tile_target, intersection):
    band_count = lax.axis_size("space")
    position = lax.axis_index("space")
    tracer = jnp.concatenate([concentration[:, :1] + emissions[:, None], concentration[:, 1:]], 1)
    east_wind = courant[0]
    north_wind = courant[1]
    edge_wind = None
    row_wind = None
    cx = None
    cy = None
    slot_hot, slot_block = slot_plan(tile_target, band_count)
    got_block = None
    for step_number in range(2):
        padded, cx, edge_wind, rode = column_halos(
            tracer,
            east_wind,
            north_wind,
            position,
            band_count,
            edge_wind,
            cx,
        )
        tracer = parabola_sweep(padded, cx, 4)
        padded, cy, row_wind, rode = row_halos(
            tracer,
            east_wind,
            north_wind,
            position,
            band_count,
            row_wind,
            cy,
            slot_block if step_number == 1 else None,
        )
        if step_number == 1:
            got_block = rode
        tracer = parabola_sweep(padded, cy, 3)
    regridded = regrid(tracer, tile_source, slot_hot, got_block, intersection, band_count)
    ensemble_moments = moments_of(regridded)
    return (tracer, regridded, ensemble_moments)


def solution(mesh):
    return jax.shard_map(
        local,
        mesh=mesh,
        in_specs=(
            P("scen", None, None, "space", None),
            P("scen", None, "space", None),
            P(None, None, None, "space", None),
            P("space"),
            P("space"),
            P("space", None, None),
        ),
        out_specs=(
            P("scen", None, None, "space", None),
            P("scen", None, "space", None),
            P(None, None, "space", None),
        ),
        check_vma=False,
    )
```
